256 devices in a mesh: seq: 64 (over y, z, core), tp: 4 (over x).
Axes of the slice: x: 4, y: 4, z: 8, core: 2. Of those that a mesh axis runs over, the one named last changes fastest.
Arguments:
- tokens: bfloat16 [512, 1152], P('seq'), may hold values from -6 to 6
- attn_gain: float32 [1152], replicated, may hold values from 0.1 to 1.9
- w_query: bfloat16 [1152, 1280], P(None, 'tp'), may hold values from -0.1875 to 0.1875
- w_key: bfloat16 [1152, 384], replicated, may hold values from -0.1875 to 0.1875
- w_value: bfloat16 [1152, 384], replicated, may hold values from -0.1875 to 0.1875
- w_out: bfloat16 [1280, 1152], P('tp'), may hold values from -0.1875 to 0.1875
- prefix_keys: bfloat16 [8, 32768, 384], P(None, 'seq'), may hold values from -92 to 92
- prefix_values: bfloat16 [8, 32768, 384], P(None, 'seq'), may hold values from -6 to 6
- suffix_keys: bfloat16 [512, 128, 384], P('seq'), may hold values from -92 to 92
- suffix_values: bfloat16 [512, 128, 384], P('seq'), may hold values from -6 to 6
- group_of: int32 [512], replicated, may hold values from 0 to 7, as said below
- prefix_len: int32 [8], replicated, may hold values from 1 to 32768, as said below
- suffix_len: int32 [512], replicated, may hold values from 0 to 128, as said below
- mlp_gain: float32 [1152], replicated, may hold values from 0.1 to 1.9
- w_gate: bfloat16 [1152, 3072], P(None, 'tp'), may hold values from -0.1875 to 0.1875
- w_up: bfloat16 [1152, 3072], P(None, 'tp'), may hold values from -0.1875 to 0.1875
- w_down: bfloat16 [3072, 1152], P('tp'), may hold values from -0.109375 to 0.109375
Outputs:
- layer_out: bfloat16 [512, 1152], P('seq')
The draws below stay inside these ranges and needn't reach their ends.
Inputs may be any that keep to these rules, and one draw needn't show every extreme that they name: `group_of`: prompt group of each request; every request reads its group's stored prefix. `prefix_len`: stored prefix positions in use for each group. `suffix_len`: stored suffix positions in use for each request.
All inputs are finite; a program needn't handle non-finite values.
Results may differ from the reference program's by a relative error of at most 0.018.
Values may be sent and summed in bfloat16 or wider, within the bound.
No kernel may reach another device: no remote copies, remote signals or barrier semaphores. Data moves between devices by JAX's collectives and lax.ppermute only.
A program may use at most 192 MiB of HBM per device.

```python
import jax
import jax.numpy as jnp
import numpy as np
from jax import lax

D = 1152
HEADS = 18
KV_HEADS = 6
HD = 64
FF = 3072
SLEN = 128
GROUPS = 8
SLOTS = 5
QCOLS = 1280
REQ = 512
PLEN = 32768
N_TP = 4


def pinned(base_key, item_count, lowest, highest):
    drawn = jax.random.randint(base_key, (item_count,), lowest, highest + 1, jnp.int32)
    chosen = jax.random.randint(jax.random.fold_in(base_key, 3), (), 0, item_count, jnp.int32)
    drawn = drawn.at[chosen].set(highest)
    return drawn.at[(chosen + 1) % item_count].set(lowest)


def draw_group_of(key, part):
    return pinned(key, REQ, 0, GROUPS - 1)


def draw_prefix_len(key, part):
    return pinned(key, GROUPS, 1, PLEN)


def draw_suffix_len(key, part):
    return pinned(key, REQ, 0, SLEN)


def draw_prefix_keys(key, part):
    shape_all = (GROUPS, PLEN, KV_HEADS * HD)
    return (3.0 * jnp.clip(jax.random.normal(key, shape_all, jnp.float32), -5.0, 5.0)).astype(jnp.bfloat16)


def draw_suffix_keys(key, part):
    shape_all = (REQ, SLEN, KV_HEADS * HD)
    return (3.0 * jnp.clip(jax.random.normal(key, shape_all, jnp.float32), -5.0, 5.0)).astype(jnp.bfloat16)


def steps_of(rng, dims, split, low, high):
    gain, own = 1.0, jax.random.fold_in(rng, 6)
    for dim, blocks in split:
        heights = jnp.exp(jax.random.uniform(jax.random.fold_in(own, dim), (blocks,), jnp.float32, low / len(split), high / len(split)))
        gain = gain * jnp.repeat(heights, dims[dim] // blocks).reshape([-1 if axis == dim else 1 for axis in range(len(dims))])
    return gain


def scatter_about(rng, extent, width, bound, shards=(), kind=jnp.bfloat16):
    level = steps_of(rng, extent, shards, -0.22, 0.18) if shards else 1.0
    values = jax.random.normal(rng, extent, jnp.float32) * width * level
    return jnp.minimum(jnp.maximum(values, -bound), bound).astype(kind)


def setup_inputs(seed: int = 0) -> dict:
    splits = jax.random.split(jax.random.key(seed), 18)
    tokens = scatter_about(splits[0], (REQ, D), 1.0, 6.0, ((0, 64),))
    attn_gain = jnp.clip(1.0 + 0.18 * jax.random.normal(splits[1], (D,), jnp.float32), 0.1, 1.9)
    w_query = scatter_about(splits[2], (D, QCOLS), D ** -0.5, 0.1875, ((1, 4),))
    w_key = scatter_about(splits[3], (D, KV_HEADS * HD), D ** -0.5, 0.1875)
    w_value = scatter_about(splits[4], (D, KV_HEADS * HD), D ** -0.5, 0.1875)
    w_out = scatter_about(splits[5], (QCOLS, D), (HEADS * HD) ** -0.5, 0.1875, ((0, 4),))
    prefix_keys = draw_prefix_keys(jax.random.fold_in(splits[17], 71), 0)
    prefix_values = scatter_about(splits[7], (GROUPS, PLEN, KV_HEADS * HD), 1.0, 6.0, ((1, 64),))
    suffix_keys = draw_suffix_keys(jax.random.fold_in(splits[17], 71), 0)
    suffix_values = scatter_about(splits[9], (REQ, SLEN, KV_HEADS * HD), 1.0, 6.0, ((0, 64),))
    group_of = draw_group_of(jax.random.fold_in(splits[17], 71), 0)
    prefix_len = draw_prefix_len(jax.random.fold_in(splits[17], 71), 0)
    suffix_len = draw_suffix_len(jax.random.fold_in(splits[17], 71), 0)
    mlp_gain = jnp.clip(1.0 + 0.18 * jax.random.normal(splits[13], (D,), jnp.float32), 0.1, 1.9)
    w_gate = scatter_about(splits[14], (D, FF), D ** -0.5, 0.1875, ((1, 4),))
    w_up = scatter_about(splits[15], (D, FF), D ** -0.5, 0.1875, ((1, 4),))
    w_down = scatter_about(splits[16], (FF, D), FF ** -0.5, 0.109375, ((0, 4),))
    return dict(tokens=tokens, attn_gain=attn_gain, w_query=w_query, w_key=w_key, w_value=w_value, w_out=w_out, prefix_keys=prefix_keys, prefix_values=prefix_values, suffix_keys=suffix_keys, suffix_values=suffix_values, group_of=group_of, prefix_len=prefix_len, suffix_len=suffix_len, mlp_gain=mlp_gain, w_gate=w_gate, w_up=w_up, w_down=w_down)


NEG_FILL = -1e+30

def rms_scale(values_in, gain_row):
    widened = values_in.astype(jnp.float32)
    factor = lax.rsqrt(lax.optimization_barrier(jnp.mean(widened * widened, axis=-1, keepdims=True)) + 1e-05)
    return (widened * factor * gain_row).astype(jnp.bfloat16)

def rotate_heads(blocks, position):
    half_dim = blocks.shape[-1] // 2
    frequency = jnp.power(10000.0, -jnp.arange(half_dim, dtype=jnp.float32) / half_dim)
    angles = position.astype(jnp.float32)[:, None, None] * frequency
    cosine = jnp.cos(angles)
    sine_part = jnp.sin(angles)
    low_half = blocks[..., :half_dim]
    high_half = blocks[..., half_dim:]
    return jnp.concatenate([low_half * cosine - high_half * sine_part, high_half * cosine + low_half * sine_part], axis=-1)

def slot_tables():
    per_device = HEADS // N_TP
    surplus = HEADS % N_TP
    slot_ids = np.arange(N_TP * SLOTS)
    device_ids = slot_ids // SLOTS
    within_ids = slot_ids % SLOTS
    head_ids = per_device * device_ids + np.minimum(device_ids, surplus) + within_ids
    slot_used = within_ids < per_device + (device_ids < surplus)
    kv_table = np.minimum(head_ids, HEADS - 1) // (HEADS // KV_HEADS)
    return (kv_table.astype(np.int32), slot_used.astype(np.float32))

def reference(tokens, attn_gain, w_query, w_key, w_value, w_out, prefix_keys, prefix_values, suffix_keys, suffix_values, group_of, prefix_len, suffix_len, mlp_gain, w_gate, w_up, w_down):
    kv_table, used_table = slot_tables()
    kv_ids = jnp.asarray(kv_table, jnp.int32)
    slot_used = jnp.asarray(used_table, jnp.float32)
    slot_total = kv_table.shape[0]
    normed = rms_scale(tokens, attn_gain)
    queries = jnp.dot(normed, w_query, preferred_element_type=jnp.float32).reshape(REQ, slot_total, HD)
    new_keys = jnp.dot(normed, w_key, preferred_element_type=jnp.float32).reshape(REQ, KV_HEADS, HD)
    new_values = jnp.dot(normed, w_value, preferred_element_type=jnp.float32).astype(jnp.bfloat16).reshape(REQ, KV_HEADS, HD)
    own_prefix = jnp.take(prefix_len, group_of)
    position = own_prefix + suffix_len
    queries = rotate_heads(queries, position).astype(jnp.bfloat16)
    new_keys = rotate_heads(new_keys, position).astype(jnp.bfloat16)
    score_scale = HD ** (-0.5)
    spots = jnp.arange(PLEN + SLEN, dtype=jnp.int32)

    def one_request(request_items):
        query_row, key_row, value_row, group_id, prefix_live, suffix_live, suffix_key_rows, suffix_value_rows = request_items
        prefix_key_rows = lax.dynamic_index_in_dim(prefix_keys, group_id, 0, keepdims=False)
        prefix_value_rows = lax.dynamic_index_in_dim(prefix_values, group_id, 0, keepdims=False)
        keys_all = jnp.concatenate([prefix_key_rows, suffix_key_rows], axis=0).reshape(-1, KV_HEADS, HD)
        values_all = jnp.concatenate([prefix_value_rows, suffix_value_rows], axis=0).reshape(-1, KV_HEADS, HD)
        keys_slot = jnp.take(keys_all, kv_ids, axis=1).astype(jnp.float32)
        values_slot = jnp.take(values_all, kv_ids, axis=1).astype(jnp.float32)
        query_wide = query_row.astype(jnp.float32)
        scores = jnp.einsum('sd,psd->sp', query_wide, keys_slot) * score_scale
        own_score = lax.optimization_barrier(jnp.sum(query_wide * jnp.take(key_row, kv_ids, axis=0).astype(jnp.float32), axis=-1)) * score_scale
        live = jnp.where(spots < PLEN, spots < prefix_live, spots - PLEN < suffix_live)
        top_score = jnp.maximum(lax.optimization_barrier(jnp.max(jnp.where(live[None, :], scores, NEG_FILL), axis=1)), own_score)
        weights = jnp.where(live[None, :], jnp.exp(scores - top_score[:, None]), 0.0)
        own_weight = jnp.exp(own_score - top_score)
        denominator = lax.optimization_barrier(jnp.sum(weights, axis=1)) + own_weight
        weights_low = lax.optimization_barrier(weights.astype(jnp.bfloat16)).astype(jnp.float32)
        own_low = lax.optimization_barrier(own_weight.astype(jnp.bfloat16)).astype(jnp.float32)
        numerator = jnp.einsum('sp,psd->sd', weights_low, values_slot)
        numerator = numerator + own_low[:, None] * jnp.take(value_row, kv_ids, axis=0).astype(jnp.float32)
        return (numerator / denominator[:, None] * slot_used[:, None]).astype(jnp.bfloat16)
    attended = lax.map(one_request, (queries, new_keys, new_values, group_of, own_prefix, suffix_len, suffix_keys, suffix_values))
    head_total = jnp.dot(attended.reshape(REQ, slot_total * HD), w_out, preferred_element_type=jnp.float32)
    hidden = (tokens.astype(jnp.float32) + head_total).astype(jnp.bfloat16)
    mlp_in = rms_scale(hidden, mlp_gain)
    gate_part = jnp.dot(mlp_in, w_gate, preferred_element_type=jnp.float32)
    up_part = jnp.dot(mlp_in, w_up, preferred_element_type=jnp.float32)
    activation = (jax.nn.silu(gate_part) * up_part).astype(jnp.bfloat16)
    down_total = jnp.dot(activation, w_down, preferred_element_type=jnp.float32)
    return (hidden.astype(jnp.float32) + down_total).astype(jnp.bfloat16)
```

```python
import jax
import jax.numpy as jnp
from jax import lax
from jax.sharding import PartitionSpec as P

HEADS = 18
KV_HEADS = 6
HD = 64


NEG_FILL = -1e30


def rms_scale(values_in, gain_row):
    widened = values_in.astype(jnp.float32)
    factor = lax.rsqrt(jnp.mean(widened * widened, axis=-1, keepdims=True) + 1e-05)
    return (widened * factor * gain_row).astype(jnp.bfloat16)


def rotate_heads(blocks, position):
    half_dim = blocks.shape[-1] // 2
    frequency = jnp.power(10000.0, -jnp.arange(half_dim, dtype=jnp.float32) / half_dim)
    angles = position.astype(jnp.float32)[:, None, None] * frequency
    cosine = jnp.cos(angles)
    sine_part = jnp.sin(angles)
    low_half = blocks[..., :half_dim]
    high_half = blocks[..., half_dim:]
    return jnp.concatenate(
        [low_half * cosine - high_half * sine_part, high_half * cosine + low_half * sine_part],
        axis=-1,
    )


def slot_layout(device_tp, tp_count, slot_count):
    per_device = HEADS // tp_count
    surplus = HEADS % tp_count
    start_head = per_device * device_tp + jnp.minimum(device_tp, surplus)
    used_count = per_device + (device_tp < surplus).astype(jnp.int32)
    slot_ids = jnp.arange(slot_count, dtype=jnp.int32)
    head_ids = start_head + slot_ids
    slot_used = (slot_ids < used_count).astype(jnp.float32)
    kv_ids = jnp.minimum(head_ids, HEADS - 1) // (HEADS // KV_HEADS)
    return (kv_ids, slot_used)


def tp_sum(part):
    pieces = lax.all_gather(part.astype(jnp.bfloat16), "tp", axis=0)
    return jnp.sum(pieces.astype(jnp.float32), axis=0)


def on_device(
    tokens,
    attn_gain,
    w_query,
    w_key,
    w_value,
    w_out,
    prefix_keys,
    prefix_values,
    suffix_keys,
    suffix_values,
    group_of,
    prefix_len,
    suffix_len,
    mlp_gain,
    w_gate,
    w_up,
    w_down,
):
    row_count = tokens.shape[0]
    slot_count = w_query.shape[1] // HD
    group_count = prefix_keys.shape[0]
    prefix_span = prefix_keys.shape[1]
    suffix_span = suffix_keys.shape[1]
    seq_index = lax.axis_index("seq")
    kv_ids, slot_used = slot_layout(lax.axis_index("tp"), lax.axis_size("tp"), slot_count)
    normed = rms_scale(tokens, attn_gain)
    queries = jnp.dot(normed, w_query, preferred_element_type=jnp.float32).reshape(
        row_count, slot_count, HD
    )
    new_keys = jnp.dot(normed, w_key, preferred_element_type=jnp.float32).reshape(
        row_count, KV_HEADS, HD
    )
    new_values = (
        jnp.dot(normed, w_value, preferred_element_type=jnp.float32)
        .astype(jnp.bfloat16)
        .reshape(row_count, KV_HEADS, HD)
    )
    own_start = seq_index * row_count
    own_groups = lax.dynamic_slice_in_dim(group_of, own_start, row_count)
    own_suffix = lax.dynamic_slice_in_dim(suffix_len, own_start, row_count)
    group_ids = jnp.arange(group_count, dtype=jnp.int32)
    own_prefix = jnp.sum(
        jnp.where(own_groups[:, None] == group_ids[None, :], prefix_len[None, :], 0), axis=1
    )
    position = own_prefix + own_suffix
    queries = rotate_heads(queries, position).astype(jnp.bfloat16)
    new_keys = rotate_heads(new_keys, position).astype(jnp.bfloat16)
    seq_count = lax.axis_size("seq")
    own_query = queries.reshape(1, row_count, slot_count * HD)
    every_query = lax.all_to_all(
        jnp.broadcast_to(own_query, (seq_count, row_count, slot_count * HD)),
        "seq",
        0,
        0,
        tiled=True,
    )
    every_query = every_query.reshape(-1, slot_count, HD)
    request_count = every_query.shape[0]
    score_scale = HD ** (-0.5)
    pre_keys = jnp.take(prefix_keys.reshape(group_count, prefix_span, KV_HEADS, HD), kv_ids, axis=2)
    pre_values = jnp.take(
        prefix_values.reshape(group_count, prefix_span, KV_HEADS, HD), kv_ids, axis=2
    )
    pre_scores = (
        jnp.einsum("rsd,gpsd->rsgp", every_query, pre_keys, preferred_element_type=jnp.float32)
        * score_scale
    )
    pre_spots = seq_index * prefix_span + jnp.arange(prefix_span, dtype=jnp.int32)
    group_match = group_of[:, None] == group_ids[None, :]
    length_match = pre_spots[None, :] < prefix_len[:, None]
    pre_live = group_match[:, None, :, None] & length_match[None, None, :, :]
    top_score = jnp.max(
        jnp.where(pre_live, pre_scores, NEG_FILL).reshape(request_count, slot_count, -1), axis=2
    )
    pre_weights = jnp.where(pre_live, jnp.exp(pre_scores - top_score[:, :, None, None]), 0.0)
    totals = jnp.sum(pre_weights, axis=(2, 3))
    mixed_sum = jnp.einsum(
        "rsgp,gpsd->rsd",
        pre_weights.astype(jnp.bfloat16),
        pre_values,
        preferred_element_type=jnp.float32,
    )
    payload = jnp.concatenate([top_score[..., None], totals[..., None], mixed_sum], axis=-1)
    payload = payload.reshape(seq_count, row_count, slot_count, HD + 2)
    gathered = lax.all_to_all(payload, "seq", 0, 0, tiled=True)
    gathered_top = gathered[..., 0]
    part_top = jnp.max(gathered_top, axis=0)
    part_scale = jnp.exp(gathered_top - part_top[None])
    part_total = jnp.sum(part_scale * gathered[..., 1], axis=0)
    part_mixed = jnp.sum(part_scale[..., None] * gathered[..., 2:], axis=0)
    suf_keys = jnp.take(suffix_keys.reshape(row_count, suffix_span, KV_HEADS, HD), kv_ids, axis=2)
    suf_values = jnp.take(
        suffix_values.reshape(row_count, suffix_span, KV_HEADS, HD), kv_ids, axis=2
    )
    suf_scores = (
        jnp.einsum("rsd,rjsd->rsj", queries, suf_keys, preferred_element_type=jnp.float32)
        * score_scale
    )
    suf_live = (jnp.arange(suffix_span, dtype=jnp.int32)[None, :] < own_suffix[:, None])[:, None, :]
    suf_top = jnp.max(jnp.where(suf_live, suf_scores, NEG_FILL), axis=2)
    own_keys = jnp.take(new_keys, kv_ids, axis=1).astype(jnp.float32)
    own_values = jnp.take(new_values, kv_ids, axis=1).astype(jnp.float32)
    own_score = jnp.sum(queries.astype(jnp.float32) * own_keys, axis=-1) * score_scale
    final_top = jnp.maximum(jnp.maximum(part_top, suf_top), own_score)
    carried = jnp.exp(part_top - final_top)
    suf_weights = jnp.where(suf_live, jnp.exp(suf_scores - final_top[:, :, None]), 0.0)
    own_weight = jnp.exp(own_score - final_top)
    denominator = carried * part_total + jnp.sum(suf_weights, axis=2) + own_weight
    own_low = lax.optimization_barrier(own_weight.astype(jnp.bfloat16)).astype(jnp.float32)
    numerator = carried[..., None] * part_mixed + own_low[..., None] * own_values
    numerator = numerator + jnp.einsum(
        "rsj,rjsd->rsd",
        suf_weights.astype(jnp.bfloat16),
        suf_values,
        preferred_element_type=jnp.float32,
    )
    attended = (numerator / denominator[..., None] * slot_used[None, :, None]).astype(jnp.bfloat16)
    head_part = jnp.dot(
        attended.reshape(row_count, slot_count * HD), w_out, preferred_element_type=jnp.float32
    )
    head_total = tp_sum(head_part)
    hidden = (tokens.astype(jnp.float32) + head_total).astype(jnp.bfloat16)
    mlp_in = rms_scale(hidden, mlp_gain)
    gate_part = jnp.dot(mlp_in, w_gate, preferred_element_type=jnp.float32)
    up_part = jnp.dot(mlp_in, w_up, preferred_element_type=jnp.float32)
    activation = (jax.nn.silu(gate_part) * up_part).astype(jnp.bfloat16)
    down_part = jnp.dot(activation, w_down, preferred_element_type=jnp.float32)
    down_total = tp_sum(down_part)
    return (hidden.astype(jnp.float32) + down_total).astype(jnp.bfloat16)


def solution(mesh):
    return jax.shard_map(
        on_device,
        mesh=mesh,
        in_specs=(
            P("seq", None),
            P(),
            P(None, "tp"),
            P(),
            P(),
            P("tp", None),
            P(None, "seq", None),
            P(None, "seq", None),
            P("seq", None, None),
            P("seq", None, None),
            P(),
            P(),
            P(),
            P(),
            P(None, "tp"),
            P(None, "tp"),
            P("tp", None),
        ),
        out_specs=P("seq", None),
        check_vma=False,
    )
```

```python
import jax
import jax.numpy as jnp
from jax import lax
from jax.experimental import pallas as pl
from jax.experimental.pallas import tpu as pltpu
from jax.sharding import PartitionSpec as P

HEADS = 18
KV_HEADS = 6
HD = 64


NEG_FILL = -1e30
TILE = 64


def prefix_kernel(tile_of, group_at, valid, limit, q_ref, rg_ref, cm_ref, k_ref, v_ref, m_ref, l_ref, a_ref):
    step = pl.program_id(0)
    tile = tile_of[step]
    first = jnp.logical_or(step == 0, tile_of[jnp.maximum(step - 1, 0)] != tile)

    @pl.when(first)
    def _():
        m_ref[...] = jnp.full(m_ref.shape, NEG_FILL, jnp.float32)
        l_ref[...] = jnp.zeros(l_ref.shape, jnp.float32)
        a_ref[...] = jnp.zeros(a_ref.shape, jnp.float32)

    group = group_at[step]
    live_count = limit[group]

    @pl.when(jnp.logical_and(valid[step] == 1, live_count > 0))
    def _():
        scores = lax.dot_general(
            q_ref[...], k_ref[0], (((1,), (1,)), ((), ())), preferred_element_type=jnp.float32
        ) * (HD ** (-0.5))
        row_live = rg_ref[...] == group
        spots = lax.broadcasted_iota(jnp.int32, scores.shape, 1)
        live = jnp.logical_and(spots < live_count, row_live)
        top = jnp.max(jnp.where(live, scores, NEG_FILL), axis=1, keepdims=True)
        weights = jnp.where(live, jnp.exp(scores - top), 0.0)
        total = jnp.sum(weights, axis=1, keepdims=True)
        mixed = jnp.dot(weights.astype(jnp.bfloat16), v_ref[0], preferred_element_type=jnp.float32)
        mixed = mixed * cm_ref[...]
        lanes = a_ref.shape[1]
        folded = mixed[:, 0:lanes]
        for block in range(1, mixed.shape[1] // lanes):
            folded = folded + mixed[:, block * lanes : (block + 1) * lanes]
        m_ref[...] = jnp.where(row_live, top, m_ref[...])
        l_ref[...] = jnp.where(row_live, total, l_ref[...])
        a_ref[...] = jnp.where(row_live, folded, a_ref[...])


def prefix_partials(every_query, group_of, prefix_len, seq_index, prefix_keys, prefix_values, kv_ids):
    request_count, slot_count, _ = every_query.shape
    group_count, prefix_span, width = prefix_keys.shape
    tile_count = request_count // TILE
    visit_count = tile_count + group_count - 1
    order_key = group_of * request_count + jnp.arange(request_count, dtype=jnp.int32)
    rank = jnp.sum((order_key[None, :] < order_key[:, None]).astype(jnp.int32), axis=1)
    spots = jnp.arange(request_count, dtype=jnp.int32)
    perm = jnp.sum(
        jnp.where(rank[None, :] == spots[:, None], spots[None, :], 0), axis=1
    )
    sorted_groups = jnp.take(group_of, perm)
    sorted_query = jnp.take(every_query, perm, axis=0)
    low = sorted_groups[0::TILE]
    high = sorted_groups[TILE - 1 :: TILE]
    spans = high - low + 1
    ends = jnp.cumsum(spans)
    starts = ends - spans
    visits = jnp.arange(visit_count, dtype=jnp.int32)
    tile_of = jnp.minimum(jnp.sum((ends[None, :] <= visits[:, None]).astype(jnp.int32), axis=1), tile_count - 1)
    valid = (visits < ends[-1]).astype(jnp.int32)
    group_at = jnp.where(valid == 1, jnp.take(low, tile_of) + visits - jnp.take(starts, tile_of), high[-1])
    limit = jnp.clip(prefix_len - seq_index * prefix_span, 0, prefix_span).astype(jnp.int32)
    head_blocks = width // HD
    col_block = jnp.arange(width, dtype=jnp.int32) // HD
    in_block = col_block[None, :] == kv_ids[:, None]
    padded = jnp.where(
        in_block[None], jnp.tile(sorted_query, (1, 1, head_blocks)), jnp.zeros((), sorted_query.dtype)
    ).reshape(request_count * slot_count, width)
    row_groups = jnp.repeat(sorted_groups, slot_count).reshape(-1, 1)
    col_mask = jnp.tile(in_block.astype(jnp.float32), (TILE, 1))
    rows = TILE * slot_count
    lanes = 128
    grid_spec = pltpu.PrefetchScalarGridSpec(
        num_scalar_prefetch=4,
        grid=(visit_count,),
        in_specs=[
            pl.BlockSpec((rows, width), lambda i, t, g, ok, lim: (t[i], 0)),
            pl.BlockSpec((rows, 1), lambda i, t, g, ok, lim: (t[i], 0)),
            pl.BlockSpec((rows, width), lambda i, t, g, ok, lim: (0, 0)),
            pl.BlockSpec((1, prefix_span, width), lambda i, t, g, ok, lim: (g[i], 0, 0)),
            pl.BlockSpec((1, prefix_span, width), lambda i, t, g, ok, lim: (g[i], 0, 0)),
        ],
        out_specs=[
            pl.BlockSpec((rows, 1), lambda i, t, g, ok, lim: (t[i], 0)),
            pl.BlockSpec((rows, 1), lambda i, t, g, ok, lim: (t[i], 0)),
            pl.BlockSpec((rows, lanes), lambda i, t, g, ok, lim: (t[i], 0)),
        ],
    )
    flops = visit_count * 4 * rows * width * prefix_span
    top, total, mixed = pl.pallas_call(
        prefix_kernel,
        grid_spec=grid_spec,
        out_shape=[
            jax.ShapeDtypeStruct((request_count * slot_count, 1), jnp.float32),
            jax.ShapeDtypeStruct((request_count * slot_count, 1), jnp.float32),
            jax.ShapeDtypeStruct((request_count * slot_count, lanes), jnp.float32),
        ],
        compiler_params=pltpu.CompilerParams(dimension_semantics=("arbitrary",)),
        cost_estimate=pl.CostEstimate(
            flops=flops,
            transcendentals=visit_count * rows * prefix_span,
            bytes_accessed=visit_count * 2 * prefix_span * width * 2 + request_count * slot_count * width * 2,
        ),
    )(tile_of, group_at, valid, limit, padded, row_groups, col_mask, prefix_keys, prefix_values)
    top = jnp.take(top.reshape(request_count, slot_count), rank, axis=0)
    total = jnp.take(total.reshape(request_count, slot_count), rank, axis=0)
    mixed = mixed.reshape(request_count, slot_count, lanes)
    mixed = jnp.where((kv_ids % 2 == 0)[None, :, None], mixed[..., :HD], mixed[..., HD : 2 * HD])
    mixed = jnp.take(mixed, rank, axis=0)
    return top, total, mixed


def rms_scale(values_in, gain_row):
    widened = values_in.astype(jnp.float32)
    factor = lax.rsqrt(jnp.mean(widened * widened, axis=-1, keepdims=True) + 1e-05)
    return (widened * factor * gain_row).astype(jnp.bfloat16)


def rotate_heads(blocks, position):
    half_dim = blocks.shape[-1] // 2
    frequency = jnp.power(10000.0, -jnp.arange(half_dim, dtype=jnp.float32) / half_dim)
    angles = position.astype(jnp.float32)[:, None, None] * frequency
    cosine = jnp.cos(angles)
    sine_part = jnp.sin(angles)
    low_half = blocks[..., :half_dim]
    high_half = blocks[..., half_dim:]
    return jnp.concatenate(
        [low_half * cosine - high_half * sine_part, high_half * cosine + low_half * sine_part],
        axis=-1,
    )


def slot_layout(device_tp, tp_count, slot_count):
    per_device = HEADS // tp_count
    surplus = HEADS % tp_count
    start_head = per_device * device_tp + jnp.minimum(device_tp, surplus)
    used_count = per_device + (device_tp < surplus).astype(jnp.int32)
    slot_ids = jnp.arange(slot_count, dtype=jnp.int32)
    head_ids = start_head + slot_ids
    slot_used = (slot_ids < used_count).astype(jnp.float32)
    kv_ids = jnp.minimum(head_ids, HEADS - 1) // (HEADS // KV_HEADS)
    return (kv_ids, slot_used)


def tp_sum(part):
    pieces = lax.all_gather(part.astype(jnp.bfloat16), "tp", axis=0)
    return jnp.sum(pieces.astype(jnp.float32), axis=0)


def on_device(
    tokens,
    attn_gain,
    w_query,
    w_key,
    w_value,
    w_out,
    prefix_keys,
    prefix_values,
    suffix_keys,
    suffix_values,
    group_of,
    prefix_len,
    suffix_len,
    mlp_gain,
    w_gate,
    w_up,
    w_down,
):
    row_count = tokens.shape[0]
    slot_count = w_query.shape[1] // HD
    group_count = prefix_keys.shape[0]
    prefix_span = prefix_keys.shape[1]
    suffix_span = suffix_keys.shape[1]
    seq_index = lax.axis_index("seq")
    kv_ids, slot_used = slot_layout(lax.axis_index("tp"), lax.axis_size("tp"), slot_count)
    normed = rms_scale(tokens, attn_gain)
    queries = jnp.dot(normed, w_query, preferred_element_type=jnp.float32).reshape(
        row_count, slot_count, HD
    )
    new_keys = jnp.dot(normed, w_key, preferred_element_type=jnp.float32).reshape(
        row_count, KV_HEADS, HD
    )
    new_values = (
        jnp.dot(normed, w_value, preferred_element_type=jnp.float32)
        .astype(jnp.bfloat16)
        .reshape(row_count, KV_HEADS, HD)
    )
    own_start = seq_index * row_count
    own_groups = lax.dynamic_slice_in_dim(group_of, own_start, row_count)
    own_suffix = lax.dynamic_slice_in_dim(suffix_len, own_start, row_count)
    group_ids = jnp.arange(group_count, dtype=jnp.int32)
    own_prefix = jnp.sum(
        jnp.where(own_groups[:, None] == group_ids[None, :], prefix_len[None, :], 0), axis=1
    )
    position = own_prefix + own_suffix
    queries = rotate_heads(queries, position).astype(jnp.bfloat16)
    new_keys = rotate_heads(new_keys, position).astype(jnp.bfloat16)
    seq_count = lax.axis_size("seq")
    own_query = queries.reshape(1, row_count, slot_count * HD)
    every_query = lax.all_to_all(
        jnp.broadcast_to(own_query, (seq_count, row_count, slot_count * HD)),
        "seq",
        0,
        0,
        tiled=True,
    )
    every_query = every_query.reshape(-1, slot_count, HD)
    score_scale = HD ** (-0.5)
    top_score, totals, mixed_sum = prefix_partials(
        every_query, group_of, prefix_len, seq_index, prefix_keys, prefix_values, kv_ids
    )
    payload = jnp.concatenate([top_score[..., None], totals[..., None], mixed_sum], axis=-1)
    payload = payload.reshape(seq_count, row_count, slot_count, HD + 2)
    gathered = lax.all_to_all(payload, "seq", 0, 0, tiled=True)
    gathered_top = gathered[..., 0]
    part_top = jnp.max(gathered_top, axis=0)
    part_scale = jnp.exp(gathered_top - part_top[None])
    part_total = jnp.sum(part_scale * gathered[..., 1], axis=0)
    part_mixed = jnp.sum(part_scale[..., None] * gathered[..., 2:], axis=0)
    suf_keys = jnp.take(suffix_keys.reshape(row_count, suffix_span, KV_HEADS, HD), kv_ids, axis=2)
    suf_values = jnp.take(
        suffix_values.reshape(row_count, suffix_span, KV_HEADS, HD), kv_ids, axis=2
    )
    suf_scores = (
        jnp.einsum("rsd,rjsd->rsj", queries, suf_keys, preferred_element_type=jnp.float32)
        * score_scale
    )
    suf_live = (jnp.arange(suffix_span, dtype=jnp.int32)[None, :] < own_suffix[:, None])[:, None, :]
    suf_top = jnp.max(jnp.where(suf_live, suf_scores, NEG_FILL), axis=2)
    own_keys = jnp.take(new_keys, kv_ids, axis=1).astype(jnp.float32)
    own_values = jnp.take(new_values, kv_ids, axis=1).astype(jnp.float32)
    own_score = jnp.sum(queries.astype(jnp.float32) * own_keys, axis=-1) * score_scale
    final_top = jnp.maximum(jnp.maximum(part_top, suf_top), own_score)
    carried = jnp.exp(part_top - final_top)
    suf_weights = jnp.where(suf_live, jnp.exp(suf_scores - final_top[:, :, None]), 0.0)
    own_weight = jnp.exp(own_score - final_top)
    denominator = carried * part_total + jnp.sum(suf_weights, axis=2) + own_weight
    own_low = lax.optimization_barrier(own_weight.astype(jnp.bfloat16)).astype(jnp.float32)
    numerator = carried[..., None] * part_mixed + own_low[..., None] * own_values
    numerator = numerator + jnp.einsum(
        "rsj,rjsd->rsd",
        suf_weights.astype(jnp.bfloat16),
        suf_values,
        preferred_element_type=jnp.float32,
    )
    attended = (numerator / denominator[..., None] * slot_used[None, :, None]).astype(jnp.bfloat16)
    head_part = jnp.dot(
        attended.reshape(row_count, slot_count * HD), w_out, preferred_element_type=jnp.float32
    )
    head_total = tp_sum(head_part)
    hidden = (tokens.astype(jnp.float32) + head_total).astype(jnp.bfloat16)
    mlp_in = rms_scale(hidden, mlp_gain)
    gate_part = jnp.dot(mlp_in, w_gate, preferred_element_type=jnp.float32)
    up_part = jnp.dot(mlp_in, w_up, preferred_element_type=jnp.float32)
    activation = (jax.nn.silu(gate_part) * up_part).astype(jnp.bfloat16)
    down_part = jnp.dot(activation, w_down, preferred_element_type=jnp.float32)
    down_total = tp_sum(down_part)
    return (hidden.astype(jnp.float32) + down_total).astype(jnp.bfloat16)


def solution(mesh):
    return jax.shard_map(
        on_device,
        mesh=mesh,
        in_specs=(
            P("seq", None),
            P(),
            P(None, "tp"),
            P(),
            P(),
            P("tp", None),
            P(None, "seq", None),
            P(None, "seq", None),
            P("seq", None, None),
            P("seq", None, None),
            P(),
            P(),
            P(),
            P(),
            P(None, "tp"),
            P(None, "tp"),
            P("tp", None),
        ),
        out_specs=P("seq", None),
        check_vma=False,
    )
```

```python
import jax
import jax.numpy as jnp
from jax import lax
from jax.experimental import pallas as pl
from jax.experimental.pallas import tpu as pltpu
from jax.sharding import PartitionSpec as P

HEADS = 18
KV_HEADS = 6
HD = 64


NEG_FILL = -1e30
TILE = 64


def prefix_kernel(tile_of, group_at, valid, limit, kv, perm_ref, sg_ref, q_ref, k_ref, v_ref, o_ref):
    step = pl.program_id(0)
    tile = tile_of[step]
    first = jnp.logical_or(step == 0, tile_of[jnp.maximum(step - 1, 0)] != tile)
    rows, width = o_ref.shape
    lanes = 128
    slot_count = kv.shape[0]
    tail_at = (slot_count // 2) * lanes
    wide_lane = lax.broadcasted_iota(jnp.int32, (rows, width), 1)

    @pl.when(first)
    def _():
        top_lanes = jnp.logical_and(wide_lane >= tail_at + HD, wide_lane < tail_at + HD + slot_count)
        o_ref[...] = jnp.where(top_lanes, NEG_FILL, 0.0).astype(jnp.float32)

    group = group_at[step]
    live_count = limit[group]

    @pl.when(jnp.logical_and(valid[step] == 1, live_count > 0))
    def _():
        request_count = q_ref.shape[0]
        pick = (perm_ref[...] == lax.broadcasted_iota(jnp.int32, (rows, request_count), 1)).astype(jnp.bfloat16)
        q_rows = jnp.dot(pick, q_ref[...], preferred_element_type=jnp.float32)
        row_live = sg_ref[...] == group
        spots = lax.broadcasted_iota(jnp.int32, (rows, k_ref.shape[1]), 1)
        live = jnp.logical_and(spots < live_count, row_live)
        lane = lax.broadcasted_iota(jnp.int32, (rows, lanes), 1)
        upper = lane >= HD
        pieces, tops, totals = [], [], []
        for slot in range(slot_count):
            head = kv[slot]
            start = pl.multiple_of((head // 2) * lanes, lanes)
            odd = head % 2 == 1
            half = slot % 2 == 1
            block = q_rows[:, (slot // 2) * lanes : (slot // 2 + 1) * lanes]
            block = jnp.where(upper == half, block, 0.0)
            block = jnp.where(odd == half, block, pltpu.roll(block, HD, 1))
            scores = lax.dot_general(
                block.astype(jnp.bfloat16),
                k_ref[0, :, pl.ds(start, lanes)],
                (((1,), (1,)), ((), ())),
                preferred_element_type=jnp.float32,
            ) * (HD ** (-0.5))
            top = jnp.max(jnp.where(live, scores, NEG_FILL), axis=1, keepdims=True)
            weights = jnp.where(live, jnp.exp(scores - top), 0.0)
            totals.append(jnp.sum(weights, axis=1, keepdims=True))
            tops.append(top)
            mixed = jnp.dot(
                weights.astype(jnp.bfloat16), v_ref[0, :, pl.ds(start, lanes)], preferred_element_type=jnp.float32
            )
            pieces.append(jnp.where(odd == half, mixed, pltpu.roll(mixed, HD, 1)))
        if slot_count % 2:
            pieces.append(jnp.zeros((rows, lanes), jnp.float32))
        out = [jnp.where(upper, pieces[i + 1], pieces[i]) for i in range(0, len(pieces), 2)]
        tail = out[-1]
        for slot in range(slot_count):
            tail = jnp.where(lane == HD + slot, tops[slot], tail)
            tail = jnp.where(lane == HD + 8 + slot, totals[slot], tail)
        out[-1] = tail
        o_ref[...] = jnp.where(row_live, jnp.concatenate(out, axis=1), o_ref[...])


def prefix_partials(every_query, group_of, prefix_len, seq_index, prefix_keys, prefix_values, kv_ids):
    request_count, width = every_query.shape
    group_count, prefix_span, _ = prefix_keys.shape
    tile_count = request_count // TILE
    visit_count = tile_count + group_count - 1
    order_key = group_of * request_count + jnp.arange(request_count, dtype=jnp.int32)
    rank = jnp.sum((order_key[None, :] < order_key[:, None]).astype(jnp.int32), axis=1)
    spots = jnp.arange(request_count, dtype=jnp.int32)
    match = rank[None, :] == spots[:, None]
    perm = jnp.sum(jnp.where(match, spots[None, :], 0), axis=1)
    sorted_groups = jnp.sum(jnp.where(match, group_of[None, :], 0), axis=1)
    low = sorted_groups[0::TILE]
    high = sorted_groups[TILE - 1 :: TILE]
    spans = high - low + 1
    ends = jnp.cumsum(spans)
    starts = ends - spans
    visits = jnp.arange(visit_count, dtype=jnp.int32)
    tile_of = jnp.minimum(jnp.sum((ends[None, :] <= visits[:, None]).astype(jnp.int32), axis=1), tile_count - 1)
    valid = (visits < ends[-1]).astype(jnp.int32)
    group_at = jnp.where(valid == 1, jnp.take(low, tile_of) + visits - jnp.take(starts, tile_of), high[-1])
    limit = jnp.clip(prefix_len - seq_index * prefix_span, 0, prefix_span).astype(jnp.int32)
    slot_count = kv_ids.shape[0]
    grid_spec = pltpu.PrefetchScalarGridSpec(
        num_scalar_prefetch=5,
        grid=(visit_count,),
        in_specs=[
            pl.BlockSpec((TILE, 1), lambda i, t, g, ok, lim, kv: (t[i], 0)),
            pl.BlockSpec((TILE, 1), lambda i, t, g, ok, lim, kv: (t[i], 0)),
            pl.BlockSpec((request_count, width), lambda i, t, g, ok, lim, kv: (0, 0)),
            pl.BlockSpec((1, prefix_span, width), lambda i, t, g, ok, lim, kv: (g[i], 0, 0)),
            pl.BlockSpec((1, prefix_span, width), lambda i, t, g, ok, lim, kv: (g[i], 0, 0)),
        ],
        out_specs=pl.BlockSpec((TILE, width), lambda i, t, g, ok, lim, kv: (t[i], 0)),
    )
    lanes = 128
    flops = visit_count * (2 * TILE * request_count * width + slot_count * 4 * TILE * lanes * prefix_span)
    out = pl.pallas_call(
        prefix_kernel,
        grid_spec=grid_spec,
        out_shape=jax.ShapeDtypeStruct((request_count, width), jnp.float32),
        compiler_params=pltpu.CompilerParams(dimension_semantics=("arbitrary",)),
        cost_estimate=pl.CostEstimate(
            flops=flops,
            transcendentals=visit_count * TILE * slot_count * prefix_span,
            bytes_accessed=visit_count * 2 * prefix_span * width * 2 + request_count * width * 6,
        ),
    )(
        tile_of,
        group_at,
        valid,
        limit,
        kv_ids,
        perm.reshape(-1, 1),
        sorted_groups.reshape(-1, 1),
        every_query,
        prefix_keys,
        prefix_values,
    )
    return jnp.take(out, rank, axis=0)


def rms_scale(values_in, gain_row):
    widened = values_in.astype(jnp.float32)
    factor = lax.rsqrt(jnp.mean(widened * widened, axis=-1, keepdims=True) + 1e-05)
    return (widened * factor * gain_row).astype(jnp.bfloat16)


def rotate_heads(blocks, position):
    half_dim = blocks.shape[-1] // 2
    frequency = jnp.power(10000.0, -jnp.arange(half_dim, dtype=jnp.float32) / half_dim)
    angles = position.astype(jnp.float32)[:, None, None] * frequency
    cosine = jnp.cos(angles)
    sine_part = jnp.sin(angles)
    low_half = blocks[..., :half_dim]
    high_half = blocks[..., half_dim:]
    return jnp.concatenate(
        [low_half * cosine - high_half * sine_part, high_half * cosine + low_half * sine_part],
        axis=-1,
    )


def slot_layout(device_tp, tp_count, slot_count):
    per_device = HEADS // tp_count
    surplus = HEADS % tp_count
    start_head = per_device * device_tp + jnp.minimum(device_tp, surplus)
    used_count = per_device + (device_tp < surplus).astype(jnp.int32)
    slot_ids = jnp.arange(slot_count, dtype=jnp.int32)
    head_ids = start_head + slot_ids
    slot_used = (slot_ids < used_count).astype(jnp.float32)
    kv_ids = jnp.minimum(head_ids, HEADS - 1) // (HEADS // KV_HEADS)
    return (kv_ids, slot_used)


def tp_sum(part):
    pieces = lax.all_gather(part.astype(jnp.bfloat16), "tp", axis=0)
    return jnp.sum(pieces.astype(jnp.float32), axis=0)


def on_device(
    tokens,
    attn_gain,
    w_query,
    w_key,
    w_value,
    w_out,
    prefix_keys,
    prefix_values,
    suffix_keys,
    suffix_values,
    group_of,
    prefix_len,
    suffix_len,
    mlp_gain,
    w_gate,
    w_up,
    w_down,
):
    row_count = tokens.shape[0]
    slot_count = w_query.shape[1] // HD
    group_count = prefix_keys.shape[0]
    prefix_span = prefix_keys.shape[1]
    suffix_span = suffix_keys.shape[1]
    seq_index = lax.axis_index("seq")
    kv_ids, slot_used = slot_layout(lax.axis_index("tp"), lax.axis_size("tp"), slot_count)
    normed = rms_scale(tokens, attn_gain)
    queries = jnp.dot(normed, w_query, preferred_element_type=jnp.float32).reshape(
        row_count, slot_count, HD
    )
    new_keys = jnp.dot(normed, w_key, preferred_element_type=jnp.float32).reshape(
        row_count, KV_HEADS, HD
    )
    new_values = (
        jnp.dot(normed, w_value, preferred_element_type=jnp.float32)
        .astype(jnp.bfloat16)
        .reshape(row_count, KV_HEADS, HD)
    )
    own_start = seq_index * row_count
    own_groups = lax.dynamic_slice_in_dim(group_of, own_start, row_count)
    own_suffix = lax.dynamic_slice_in_dim(suffix_len, own_start, row_count)
    group_ids = jnp.arange(group_count, dtype=jnp.int32)
    own_prefix = jnp.sum(
        jnp.where(own_groups[:, None] == group_ids[None, :], prefix_len[None, :], 0), axis=1
    )
    position = own_prefix + own_suffix
    queries = rotate_heads(queries, position).astype(jnp.bfloat16)
    new_keys = rotate_heads(new_keys, position).astype(jnp.bfloat16)
    seq_count = lax.axis_size("seq")
    query_width = prefix_keys.shape[2]
    own_query = jnp.pad(
        queries.reshape(1, row_count, slot_count * HD),
        ((0, 0), (0, 0), (0, query_width - slot_count * HD)),
    )
    every_query = lax.all_to_all(
        jnp.broadcast_to(own_query, (seq_count, row_count, query_width)),
        "seq",
        0,
        0,
        tiled=True,
    )
    every_query = every_query.reshape(-1, query_width)
    score_scale = HD ** (-0.5)
    payload = prefix_partials(
        every_query, group_of, prefix_len, seq_index, prefix_keys, prefix_values, kv_ids
    )
    payload = payload.reshape(seq_count, row_count, query_width)
    gathered = lax.all_to_all(payload, "seq", 0, 0, tiled=True)
    tail_at = (slot_count // 2) * 128 + HD
    gathered_top = gathered[..., tail_at : tail_at + slot_count]
    gathered_total = gathered[..., tail_at + 8 : tail_at + 8 + slot_count]
    gathered_mixed = gathered[..., : slot_count * HD].reshape(seq_count, row_count, slot_count, HD)
    part_top = jnp.max(gathered_top, axis=0)
    part_scale = jnp.exp(gathered_top - part_top[None])
    part_total = jnp.sum(part_scale * gathered_total, axis=0)
    part_mixed = jnp.sum(part_scale[..., None] * gathered_mixed, axis=0)
    suf_keys = jnp.take(suffix_keys.reshape(row_count, suffix_span, KV_HEADS, HD), kv_ids, axis=2)
    suf_values = jnp.take(
        suffix_values.reshape(row_count, suffix_span, KV_HEADS, HD), kv_ids, axis=2
    )
    suf_scores = (
        jnp.einsum("rsd,rjsd->rsj", queries, suf_keys, preferred_element_type=jnp.float32)
        * score_scale
    )
    suf_live = (jnp.arange(suffix_span, dtype=jnp.int32)[None, :] < own_suffix[:, None])[:, None, :]
    suf_top = jnp.max(jnp.where(suf_live, suf_scores, NEG_FILL), axis=2)
    own_keys = jnp.take(new_keys, kv_ids, axis=1).astype(jnp.float32)
    own_values = jnp.take(new_values, kv_ids, axis=1).astype(jnp.float32)
    own_score = jnp.sum(queries.astype(jnp.float32) * own_keys, axis=-1) * score_scale
    final_top = jnp.maximum(jnp.maximum(part_top, suf_top), own_score)
    carried = jnp.exp(part_top - final_top)
    suf_weights = jnp.where(suf_live, jnp.exp(suf_scores - final_top[:, :, None]), 0.0)
    own_weight = jnp.exp(own_score - final_top)
    denominator = carried * part_total + jnp.sum(suf_weights, axis=2) + own_weight
    own_low = lax.optimization_barrier(own_weight.astype(jnp.bfloat16)).astype(jnp.float32)
    numerator = carried[..., None] * part_mixed + own_low[..., None] * own_values
    numerator = numerator + jnp.einsum(
        "rsj,rjsd->rsd",
        suf_weights.astype(jnp.bfloat16),
        suf_values,
        preferred_element_type=jnp.float32,
    )
    attended = (numerator / denominator[..., None] * slot_used[None, :, None]).astype(jnp.bfloat16)
    head_part = jnp.dot(
        attended.reshape(row_count, slot_count * HD), w_out, preferred_element_type=jnp.float32
    )
    head_total = tp_sum(head_part)
    hidden = (tokens.astype(jnp.float32) + head_total).astype(jnp.bfloat16)
    mlp_in = rms_scale(hidden, mlp_gain)
    gate_part = jnp.dot(mlp_in, w_gate, preferred_element_type=jnp.float32)
    up_part = jnp.dot(mlp_in, w_up, preferred_element_type=jnp.float32)
    activation = (jax.nn.silu(gate_part) * up_part).astype(jnp.bfloat16)
    down_part = jnp.dot(activation, w_down, preferred_element_type=jnp.float32)
    down_total = tp_sum(down_part)
    return (hidden.astype(jnp.float32) + down_total).astype(jnp.bfloat16)


def solution(mesh):
    return jax.shard_map(
        on_device,
        mesh=mesh,
        in_specs=(
            P("seq", None),
            P(),
            P(None, "tp"),
            P(),
            P(),
            P("tp", None),
            P(None, "seq", None),
            P(None, "seq", None),
            P("seq", None, None),
            P("seq", None, None),
            P(),
            P(),
            P(),
            P(),
            P(None, "tp"),
            P(None, "tp"),
            P("tp", None),
        ),
        out_specs=P("seq", None),
        check_vma=False,
    )
```

```python
import jax
import jax.numpy as jnp
from jax import lax
from jax.experimental import pallas as pl
from jax.experimental.pallas import tpu as pltpu
from jax.sharding import PartitionSpec as P

HEADS = 18
KV_HEADS = 6
HD = 64


NEG_FILL = -1e30
TILE = 64


def prefix_kernel(tile_of, group_at, valid, limit, kv, perm_ref, sg_ref, q_ref, k_ref, v_ref, o_ref):
    step = pl.program_id(0)
    tile = tile_of[step]
    first = jnp.logical_or(step == 0, tile_of[jnp.maximum(step - 1, 0)] != tile)
    rows, width = o_ref.shape
    lanes = 128
    slot_count = kv.shape[0]
    tail_at = (slot_count // 2) * lanes
    wide_lane = lax.broadcasted_iota(jnp.int32, (rows, width), 1)

    @pl.when(first)
    def _():
        top_lanes = jnp.logical_and(wide_lane >= tail_at + HD, wide_lane < tail_at + HD + slot_count)
        o_ref[...] = jnp.where(top_lanes, NEG_FILL, 0.0).astype(jnp.float32)

    group = group_at[step]
    live_count = limit[group]

    @pl.when(jnp.logical_and(valid[step] == 1, live_count > 0))
    def _():
        request_count = q_ref.shape[0]
        pick = (perm_ref[...] == lax.broadcasted_iota(jnp.int32, (rows, request_count), 1)).astype(jnp.bfloat16)
        q_rows = jnp.dot(pick, q_ref[...], preferred_element_type=jnp.float32)
        row_live = sg_ref[...] == group
        lane = lax.broadcasted_iota(jnp.int32, (rows, lanes), 1)
        upper = lane >= HD
        tile_total = width // lanes
        padded = []
        for slot in range(slot_count):
            head = kv[slot]
            odd = head % 2 == 1
            half = slot % 2 == 1
            block = q_rows[:, (slot // 2) * lanes : (slot // 2 + 1) * lanes]
            block = jnp.where(upper == half, block, 0.0)
            block = jnp.where(odd == half, block, pltpu.roll(block, HD, 1))
            padded.append(
                jnp.concatenate(
                    [jnp.where(head // 2 == j, block, 0.0) for j in range(tile_total)], axis=1
                ).astype(jnp.bfloat16)
            )
        padded = jnp.concatenate(padded, axis=0)
        scores = lax.dot_general(
            padded, k_ref[0], (((1,), (1,)), ((), ())), preferred_element_type=jnp.float32
        ) * (HD ** (-0.5))
        all_live = jnp.concatenate([row_live] * slot_count, axis=0)
        spots = lax.broadcasted_iota(jnp.int32, scores.shape, 1)
        live = jnp.logical_and(spots < live_count, all_live)
        top = jnp.max(jnp.where(live, scores, NEG_FILL), axis=1, keepdims=True)
        weights = jnp.where(live, jnp.exp(scores - top), 0.0)
        total = jnp.sum(weights, axis=1, keepdims=True)
        mixed = jnp.dot(weights.astype(jnp.bfloat16), v_ref[0], preferred_element_type=jnp.float32)
        pieces = []
        for slot in range(slot_count):
            head = kv[slot]
            odd = head % 2 == 1
            half = slot % 2 == 1
            mine = mixed[slot * rows : (slot + 1) * rows]
            chosen = mine[:, 0:lanes]
            for j in range(1, tile_total):
                chosen = jnp.where(head // 2 == j, mine[:, j * lanes : (j + 1) * lanes], chosen)
            pieces.append(jnp.where(odd == half, chosen, pltpu.roll(chosen, HD, 1)))
        if slot_count % 2:
            pieces.append(jnp.zeros((rows, lanes), jnp.float32))
        out = [jnp.where(upper, pieces[i + 1], pieces[i]) for i in range(0, len(pieces), 2)]
        tail = out[-1]
        for slot in range(slot_count):
            tail = jnp.where(lane == HD + slot, top[slot * rows : (slot + 1) * rows], tail)
            tail = jnp.where(lane == HD + 8 + slot, total[slot * rows : (slot + 1) * rows], tail)
        out[-1] = tail
        o_ref[...] = jnp.where(row_live, jnp.concatenate(out, axis=1), o_ref[...])


def prefix_partials(every_query, group_of, prefix_len, seq_index, prefix_keys, prefix_values, kv_ids):
    request_count, width = every_query.shape
    group_count, prefix_span, _ = prefix_keys.shape
    tile_count = request_count // TILE
    visit_count = tile_count + group_count - 1
    order_key = group_of * request_count + jnp.arange(request_count, dtype=jnp.int32)
    rank = jnp.sum((order_key[None, :] < order_key[:, None]).astype(jnp.int32), axis=1)
    spots = jnp.arange(request_count, dtype=jnp.int32)
    match = rank[None, :] == spots[:, None]
    perm = jnp.sum(jnp.where(match, spots[None, :], 0), axis=1)
    sorted_groups = jnp.sum(jnp.where(match, group_of[None, :], 0), axis=1)
    low = sorted_groups[0::TILE]
    high = sorted_groups[TILE - 1 :: TILE]
    spans = high - low + 1
    ends = jnp.cumsum(spans)
    starts = ends - spans
    visits = jnp.arange(visit_count, dtype=jnp.int32)
    tile_of = jnp.minimum(jnp.sum((ends[None, :] <= visits[:, None]).astype(jnp.int32), axis=1), tile_count - 1)
    valid = (visits < ends[-1]).astype(jnp.int32)
    group_at = jnp.where(valid == 1, jnp.take(low, tile_of) + visits - jnp.take(starts, tile_of), high[-1])
    limit = jnp.clip(prefix_len - seq_index * prefix_span, 0, prefix_span).astype(jnp.int32)
    slot_count = kv_ids.shape[0]
    grid_spec = pltpu.PrefetchScalarGridSpec(
        num_scalar_prefetch=5,
        grid=(visit_count,),
        in_specs=[
            pl.BlockSpec((TILE, 1), lambda i, t, g, ok, lim, kv: (t[i], 0)),
            pl.BlockSpec((TILE, 1), lambda i, t, g, ok, lim, kv: (t[i], 0)),
            pl.BlockSpec((request_count, width), lambda i, t, g, ok, lim, kv: (0, 0)),
            pl.BlockSpec((1, prefix_span, width), lambda i, t, g, ok, lim, kv: (g[i], 0, 0)),
            pl.BlockSpec((1, prefix_span, width), lambda i, t, g, ok, lim, kv: (g[i], 0, 0)),
        ],
        out_specs=pl.BlockSpec((TILE, width), lambda i, t, g, ok, lim, kv: (t[i], 0)),
    )
    lanes = 128
    flops = visit_count * (2 * TILE * request_count * width + slot_count * 4 * TILE * width * prefix_span)
    out = pl.pallas_call(
        prefix_kernel,
        grid_spec=grid_spec,
        out_shape=jax.ShapeDtypeStruct((request_count, width), jnp.float32),
        compiler_params=pltpu.CompilerParams(dimension_semantics=("arbitrary",)),
        cost_estimate=pl.CostEstimate(
            flops=flops,
            transcendentals=visit_count * TILE * slot_count * prefix_span,
            bytes_accessed=visit_count * 2 * prefix_span * width * 2 + request_count * width * 6,
        ),
    )(
        tile_of,
        group_at,
        valid,
        limit,
        kv_ids,
        perm.reshape(-1, 1),
        sorted_groups.reshape(-1, 1),
        every_query,
        prefix_keys,
        prefix_values,
    )
    return jnp.take(out, rank, axis=0)


def rms_scale(values_in, gain_row):
    widened = values_in.astype(jnp.float32)
    factor = lax.rsqrt(jnp.mean(widened * widened, axis=-1, keepdims=True) + 1e-05)
    return (widened * factor * gain_row).astype(jnp.bfloat16)


def rotate_heads(blocks, position):
    half_dim = blocks.shape[-1] // 2
    frequency = jnp.power(10000.0, -jnp.arange(half_dim, dtype=jnp.float32) / half_dim)
    angles = position.astype(jnp.float32)[:, None, None] * frequency
    cosine = jnp.cos(angles)
    sine_part = jnp.sin(angles)
    low_half = blocks[..., :half_dim]
    high_half = blocks[..., half_dim:]
    return jnp.concatenate(
        [low_half * cosine - high_half * sine_part, high_half * cosine + low_half * sine_part],
        axis=-1,
    )


def slot_layout(device_tp, tp_count, slot_count):
    per_device = HEADS // tp_count
    surplus = HEADS % tp_count
    start_head = per_device * device_tp + jnp.minimum(device_tp, surplus)
    used_count = per_device + (device_tp < surplus).astype(jnp.int32)
    slot_ids = jnp.arange(slot_count, dtype=jnp.int32)
    head_ids = start_head + slot_ids
    slot_used = (slot_ids < used_count).astype(jnp.float32)
    kv_ids = jnp.minimum(head_ids, HEADS - 1) // (HEADS // KV_HEADS)
    return (kv_ids, slot_used)


def tp_sum(part):
    pieces = lax.all_gather(part.astype(jnp.bfloat16), "tp", axis=0)
    return jnp.sum(pieces.astype(jnp.float32), axis=0)


def on_device(
    tokens,
    attn_gain,
    w_query,
    w_key,
    w_value,
    w_out,
    prefix_keys,
    prefix_values,
    suffix_keys,
    suffix_values,
    group_of,
    prefix_len,
    suffix_len,
    mlp_gain,
    w_gate,
    w_up,
    w_down,
):
    row_count = tokens.shape[0]
    slot_count = w_query.shape[1] // HD
    group_count = prefix_keys.shape[0]
    prefix_span = prefix_keys.shape[1]
    suffix_span = suffix_keys.shape[1]
    seq_index = lax.axis_index("seq")
    kv_ids, slot_used = slot_layout(lax.axis_index("tp"), lax.axis_size("tp"), slot_count)
    normed = rms_scale(tokens, attn_gain)
    queries = jnp.dot(normed, w_query, preferred_element_type=jnp.float32).reshape(
        row_count, slot_count, HD
    )
    new_keys = jnp.dot(normed, w_key, preferred_element_type=jnp.float32).reshape(
        row_count, KV_HEADS, HD
    )
    new_values = (
        jnp.dot(normed, w_value, preferred_element_type=jnp.float32)
        .astype(jnp.bfloat16)
        .reshape(row_count, KV_HEADS, HD)
    )
    own_start = seq_index * row_count
    own_groups = lax.dynamic_slice_in_dim(group_of, own_start, row_count)
    own_suffix = lax.dynamic_slice_in_dim(suffix_len, own_start, row_count)
    group_ids = jnp.arange(group_count, dtype=jnp.int32)
    own_prefix = jnp.sum(
        jnp.where(own_groups[:, None] == group_ids[None, :], prefix_len[None, :], 0), axis=1
    )
    position = own_prefix + own_suffix
    queries = rotate_heads(queries, position).astype(jnp.bfloat16)
    new_keys = rotate_heads(new_keys, position).astype(jnp.bfloat16)
    seq_count = lax.axis_size("seq")
    query_width = prefix_keys.shape[2]
    own_query = jnp.pad(
        queries.reshape(1, row_count, slot_count * HD),
        ((0, 0), (0, 0), (0, query_width - slot_count * HD)),
    )
    every_query = lax.all_to_all(
        jnp.broadcast_to(own_query, (seq_count, row_count, query_width)),
        "seq",
        0,
        0,
        tiled=True,
    )
    every_query = every_query.reshape(-1, query_width)
    score_scale = HD ** (-0.5)
    payload = prefix_partials(
        every_query, group_of, prefix_len, seq_index, prefix_keys, prefix_values, kv_ids
    )
    payload = payload.reshape(seq_count, row_count, query_width)
    gathered = lax.all_to_all(payload, "seq", 0, 0, tiled=True)
    tail_at = (slot_count // 2) * 128 + HD
    gathered_top = gathered[..., tail_at : tail_at + slot_count]
    gathered_total = gathered[..., tail_at + 8 : tail_at + 8 + slot_count]
    gathered_mixed = gathered[..., : slot_count * HD].reshape(seq_count, row_count, slot_count, HD)
    part_top = jnp.max(gathered_top, axis=0)
    part_scale = jnp.exp(gathered_top - part_top[None])
    part_total = jnp.sum(part_scale * gathered_total, axis=0)
    part_mixed = jnp.sum(part_scale[..., None] * gathered_mixed, axis=0)
    suf_keys = jnp.take(suffix_keys.reshape(row_count, suffix_span, KV_HEADS, HD), kv_ids, axis=2)
    suf_values = jnp.take(
        suffix_values.reshape(row_count, suffix_span, KV_HEADS, HD), kv_ids, axis=2
    )
    suf_scores = (
        jnp.einsum("rsd,rjsd->rsj", queries, suf_keys, preferred_element_type=jnp.float32)
        * score_scale
    )
    suf_live = (jnp.arange(suffix_span, dtype=jnp.int32)[None, :] < own_suffix[:, None])[:, None, :]
    suf_top = jnp.max(jnp.where(suf_live, suf_scores, NEG_FILL), axis=2)
    own_keys = jnp.take(new_keys, kv_ids, axis=1).astype(jnp.float32)
    own_values = jnp.take(new_values, kv_ids, axis=1).astype(jnp.float32)
    own_score = jnp.sum(queries.astype(jnp.float32) * own_keys, axis=-1) * score_scale
    final_top = jnp.maximum(jnp.maximum(part_top, suf_top), own_score)
    carried = jnp.exp(part_top - final_top)
    suf_weights = jnp.where(suf_live, jnp.exp(suf_scores - final_top[:, :, None]), 0.0)
    own_weight = jnp.exp(own_score - final_top)
    denominator = carried * part_total + jnp.sum(suf_weights, axis=2) + own_weight
    own_low = lax.optimization_barrier(own_weight.astype(jnp.bfloat16)).astype(jnp.float32)
    numerator = carried[..., None] * part_mixed + own_low[..., None] * own_values
    numerator = numerator + jnp.einsum(
        "rsj,rjsd->rsd",
        suf_weights.astype(jnp.bfloat16),
        suf_values,
        preferred_element_type=jnp.float32,
    )
    attended = (numerator / denominator[..., None] * slot_used[None, :, None]).astype(jnp.bfloat16)
    head_part = jnp.dot(
        attended.reshape(row_count, slot_count * HD), w_out, preferred_element_type=jnp.float32
    )
    head_total = tp_sum(head_part)
    hidden = (tokens.astype(jnp.float32) + head_total).astype(jnp.bfloat16)
    mlp_in = rms_scale(hidden, mlp_gain)
    gate_part = jnp.dot(mlp_in, w_gate, preferred_element_type=jnp.float32)
    up_part = jnp.dot(mlp_in, w_up, preferred_element_type=jnp.float32)
    activation = (jax.nn.silu(gate_part) * up_part).astype(jnp.bfloat16)
    down_part = jnp.dot(activation, w_down, preferred_element_type=jnp.float32)
    down_total = tp_sum(down_part)
    return (hidden.astype(jnp.float32) + down_total).astype(jnp.bfloat16)


def solution(mesh):
    return jax.shard_map(
        on_device,
        mesh=mesh,
        in_specs=(
            P("seq", None),
            P(),
            P(None, "tp"),
            P(),
            P(),
            P("tp", None),
            P(None, "seq", None),
            P(None, "seq", None),
            P("seq", None, None),
            P("seq", None, None),
            P(),
            P(),
            P(),
            P(),
            P(None, "tp"),
            P(None, "tp"),
            P("tp", None),
        ),
        out_specs=P("seq", None),
        check_vma=False,
    )
```

```python
import jax
import jax.numpy as jnp
from jax import lax
from jax.experimental import pallas as pl
from jax.experimental.pallas import tpu as pltpu
from jax.sharding import PartitionSpec as P

HEADS = 18
KV_HEADS = 6
HD = 64


NEG_FILL = -1e30
TILE = 64


def split_parts(values, count):
    parts = []
    for _ in range(count - 1):
        high = values.astype(jnp.bfloat16).astype(jnp.float32)
        parts.append(high)
        values = values - high
    parts.append(values.astype(jnp.bfloat16).astype(jnp.float32))
    return parts


def prefix_kernel(tile_of, group_at, valid, limit, kv, perm_ref, sg_ref, q_ref, k_ref, v_ref, o_ref):
    step = pl.program_id(0)
    tile = tile_of[step]
    first = jnp.logical_or(step == 0, tile_of[jnp.maximum(step - 1, 0)] != tile)
    rows, width = o_ref.shape
    lanes = 128
    slot_count = kv.shape[0]
    tail_at = (slot_count // 2) * lanes
    wide_lane = lax.broadcasted_iota(jnp.int32, (rows, width), 1)

    @pl.when(first)
    def _():
        top_lanes = jnp.logical_and(wide_lane >= tail_at + HD, wide_lane < tail_at + HD + slot_count)
        o_ref[...] = jnp.where(top_lanes, NEG_FILL, 0.0).astype(jnp.float32)

    group = group_at[step]
    live_count = limit[group]

    @pl.when(jnp.logical_and(valid[step] == 1, live_count > 0))
    def _():
        request_count = q_ref.shape[0]
        pick = (perm_ref[...] == lax.broadcasted_iota(jnp.int32, (rows, request_count), 1)).astype(jnp.bfloat16)
        q_rows = jnp.dot(pick, q_ref[...], preferred_element_type=jnp.float32)
        row_live = sg_ref[...] == group
        lane = lax.broadcasted_iota(jnp.int32, (rows, lanes), 1)
        upper = lane >= HD
        tile_total = width // lanes
        padded = []
        for slot in range(slot_count):
            head = kv[slot]
            odd = head % 2 == 1
            half = slot % 2 == 1
            block = q_rows[:, (slot // 2) * lanes : (slot // 2 + 1) * lanes]
            block = jnp.where(upper == half, block, 0.0)
            block = jnp.where(odd == half, block, pltpu.roll(block, HD, 1))
            padded.append(
                jnp.concatenate(
                    [jnp.where(head // 2 == j, block, 0.0) for j in range(tile_total)], axis=1
                ).astype(jnp.bfloat16)
            )
        padded = jnp.concatenate(padded, axis=0)
        scores = lax.dot_general(
            padded, k_ref[0], (((1,), (1,)), ((), ())), preferred_element_type=jnp.float32
        ) * (HD ** (-0.5))
        all_live = jnp.concatenate([row_live] * slot_count, axis=0)
        spots = lax.broadcasted_iota(jnp.int32, scores.shape, 1)
        live = jnp.logical_and(spots < live_count, all_live)
        top = jnp.max(jnp.where(live, scores, NEG_FILL), axis=1, keepdims=True)
        weights = jnp.where(live, jnp.exp(scores - top), 0.0)
        total = jnp.sum(weights, axis=1, keepdims=True)
        mixed = jnp.dot(weights.astype(jnp.bfloat16), v_ref[0], preferred_element_type=jnp.float32)
        pieces = []
        for slot in range(slot_count):
            head = kv[slot]
            odd = head % 2 == 1
            half = slot % 2 == 1
            mine = mixed[slot * rows : (slot + 1) * rows]
            chosen = mine[:, 0:lanes]
            for j in range(1, tile_total):
                chosen = jnp.where(head // 2 == j, mine[:, j * lanes : (j + 1) * lanes], chosen)
            pieces.append(jnp.where(odd == half, chosen, pltpu.roll(chosen, HD, 1)))
        if slot_count % 2:
            pieces.append(jnp.zeros((rows, lanes), jnp.float32))
        out = [jnp.where(upper, pieces[i + 1], pieces[i]) for i in range(0, len(pieces), 2)]
        tail = out[-1]
        parts = split_parts(top, 3) + split_parts(total, 3)
        for index, part in enumerate(parts):
            for slot in range(slot_count):
                tail = jnp.where(lane == HD + index * slot_count + slot, part[slot * rows : (slot + 1) * rows], tail)
        out[-1] = tail
        o_ref[...] = jnp.where(row_live, jnp.concatenate(out, axis=1), o_ref[...])


def prefix_partials(every_query, group_of, prefix_len, seq_index, prefix_keys, prefix_values, kv_ids):
    request_count, width = every_query.shape
    group_count, prefix_span, _ = prefix_keys.shape
    tile_count = request_count // TILE
    visit_count = tile_count + group_count - 1
    order_key = group_of * request_count + jnp.arange(request_count, dtype=jnp.int32)
    rank = jnp.sum((order_key[None, :] < order_key[:, None]).astype(jnp.int32), axis=1)
    spots = jnp.arange(request_count, dtype=jnp.int32)
    match = rank[None, :] == spots[:, None]
    perm = jnp.sum(jnp.where(match, spots[None, :], 0), axis=1)
    sorted_groups = jnp.sum(jnp.where(match, group_of[None, :], 0), axis=1)
    low = sorted_groups[0::TILE]
    high = sorted_groups[TILE - 1 :: TILE]
    spans = high - low + 1
    ends = jnp.cumsum(spans)
    starts = ends - spans
    visits = jnp.arange(visit_count, dtype=jnp.int32)
    tile_of = jnp.minimum(jnp.sum((ends[None, :] <= visits[:, None]).astype(jnp.int32), axis=1), tile_count - 1)
    valid = (visits < ends[-1]).astype(jnp.int32)
    group_at = jnp.where(valid == 1, jnp.take(low, tile_of) + visits - jnp.take(starts, tile_of), high[-1])
    limit = jnp.clip(prefix_len - seq_index * prefix_span, 0, prefix_span).astype(jnp.int32)
    slot_count = kv_ids.shape[0]
    grid_spec = pltpu.PrefetchScalarGridSpec(
        num_scalar_prefetch=5,
        grid=(visit_count,),
        in_specs=[
            pl.BlockSpec((TILE, 1), lambda i, t, g, ok, lim, kv: (t[i], 0)),
            pl.BlockSpec((TILE, 1), lambda i, t, g, ok, lim, kv: (t[i], 0)),
            pl.BlockSpec((request_count, width), lambda i, t, g, ok, lim, kv: (0, 0)),
            pl.BlockSpec((1, prefix_span, width), lambda i, t, g, ok, lim, kv: (g[i], 0, 0)),
            pl.BlockSpec((1, prefix_span, width), lambda i, t, g, ok, lim, kv: (g[i], 0, 0)),
        ],
        out_specs=pl.BlockSpec((TILE, width), lambda i, t, g, ok, lim, kv: (t[i], 0)),
    )
    lanes = 128
    flops = visit_count * (2 * TILE * request_count * width + slot_count * 4 * TILE * width * prefix_span)
    out = pl.pallas_call(
        prefix_kernel,
        grid_spec=grid_spec,
        out_shape=jax.ShapeDtypeStruct((request_count, width), jnp.float32),
        compiler_params=pltpu.CompilerParams(dimension_semantics=("arbitrary",)),
        cost_estimate=pl.CostEstimate(
            flops=flops,
            transcendentals=visit_count * TILE * slot_count * prefix_span,
            bytes_accessed=visit_count * 2 * prefix_span * width * 2 + request_count * width * 6,
        ),
    )(
        tile_of,
        group_at,
        valid,
        limit,
        kv_ids,
        perm.reshape(-1, 1),
        sorted_groups.reshape(-1, 1),
        every_query,
        prefix_keys,
        prefix_values,
    )
    return jnp.take(out, rank, axis=0).astype(jnp.bfloat16)


def rms_scale(values_in, gain_row):
    widened = values_in.astype(jnp.float32)
    factor = lax.rsqrt(jnp.mean(widened * widened, axis=-1, keepdims=True) + 1e-05)
    return (widened * factor * gain_row).astype(jnp.bfloat16)


def rotate_heads(blocks, position):
    half_dim = blocks.shape[-1] // 2
    frequency = jnp.power(10000.0, -jnp.arange(half_dim, dtype=jnp.float32) / half_dim)
    angles = position.astype(jnp.float32)[:, None, None] * frequency
    cosine = jnp.cos(angles)
    sine_part = jnp.sin(angles)
    low_half = blocks[..., :half_dim]
    high_half = blocks[..., half_dim:]
    return jnp.concatenate(
        [low_half * cosine - high_half * sine_part, high_half * cosine + low_half * sine_part],
        axis=-1,
    )


def slot_layout(device_tp, tp_count, slot_count):
    per_device = HEADS // tp_count
    surplus = HEADS % tp_count
    start_head = per_device * device_tp + jnp.minimum(device_tp, surplus)
    used_count = per_device + (device_tp < surplus).astype(jnp.int32)
    slot_ids = jnp.arange(slot_count, dtype=jnp.int32)
    head_ids = start_head + slot_ids
    slot_used = (slot_ids < used_count).astype(jnp.float32)
    kv_ids = jnp.minimum(head_ids, HEADS - 1) // (HEADS // KV_HEADS)
    return (kv_ids, slot_used)


def tp_sum(part):
    sent = part.astype(jnp.bfloat16)
    count = lax.axis_size("tp")
    total = sent.astype(jnp.float32)
    for shift in range(1, count):
        moved = lax.ppermute(sent, "tp", [(j, (j + shift) % count) for j in range(count)])
        total = total + moved.astype(jnp.float32)
    return total


def on_device(
    tokens,
    attn_gain,
    w_query,
    w_key,
    w_value,
    w_out,
    prefix_keys,
    prefix_values,
    suffix_keys,
    suffix_values,
    group_of,
    prefix_len,
    suffix_len,
    mlp_gain,
    w_gate,
    w_up,
    w_down,
):
    row_count = tokens.shape[0]
    slot_count = w_query.shape[1] // HD
    group_count = prefix_keys.shape[0]
    prefix_span = prefix_keys.shape[1]
    suffix_span = suffix_keys.shape[1]
    seq_index = lax.axis_index("seq")
    kv_ids, slot_used = slot_layout(lax.axis_index("tp"), lax.axis_size("tp"), slot_count)
    normed = rms_scale(tokens, attn_gain)
    queries = jnp.dot(normed, w_query, preferred_element_type=jnp.float32).reshape(
        row_count, slot_count, HD
    )
    new_keys = jnp.dot(normed, w_key, preferred_element_type=jnp.float32).reshape(
        row_count, KV_HEADS, HD
    )
    new_values = (
        jnp.dot(normed, w_value, preferred_element_type=jnp.float32)
        .astype(jnp.bfloat16)
        .reshape(row_count, KV_HEADS, HD)
    )
    own_start = seq_index * row_count
    own_groups = lax.dynamic_slice_in_dim(group_of, own_start, row_count)
    own_suffix = lax.dynamic_slice_in_dim(suffix_len, own_start, row_count)
    group_ids = jnp.arange(group_count, dtype=jnp.int32)
    own_prefix = jnp.sum(
        jnp.where(own_groups[:, None] == group_ids[None, :], prefix_len[None, :], 0), axis=1
    )
    position = own_prefix + own_suffix
    queries = rotate_heads(queries, position).astype(jnp.bfloat16)
    new_keys = rotate_heads(new_keys, position).astype(jnp.bfloat16)
    seq_count = lax.axis_size("seq")
    query_width = prefix_keys.shape[2]
    own_query = jnp.pad(
        queries.reshape(1, row_count, slot_count * HD),
        ((0, 0), (0, 0), (0, query_width - slot_count * HD)),
    )
    every_query = lax.all_to_all(
        jnp.broadcast_to(own_query, (seq_count, row_count, query_width)),
        "seq",
        0,
        0,
        tiled=True,
    )
    every_query = every_query.reshape(-1, query_width)
    score_scale = HD ** (-0.5)
    payload = prefix_partials(
        every_query, group_of, prefix_len, seq_index, prefix_keys, prefix_values, kv_ids
    )
    payload = payload.reshape(seq_count, row_count, query_width)
    gathered = lax.all_to_all(payload, "seq", 0, 0, tiled=True).astype(jnp.float32)
    tail_at = (slot_count // 2) * 128 + HD
    tail_parts = [gathered[..., tail_at + i * slot_count : tail_at + (i + 1) * slot_count] for i in range(6)]
    gathered_top = (tail_parts[0] + tail_parts[1]) + tail_parts[2]
    gathered_total = (tail_parts[3] + tail_parts[4]) + tail_parts[5]
    gathered_mixed = gathered[..., : slot_count * HD].reshape(seq_count, row_count, slot_count, HD)
    part_top = jnp.max(gathered_top, axis=0)
    part_scale = jnp.exp(gathered_top - part_top[None])
    part_total = jnp.sum(part_scale * gathered_total, axis=0)
    part_mixed = jnp.sum(part_scale[..., None] * gathered_mixed, axis=0)
    suf_keys = jnp.take(suffix_keys.reshape(row_count, suffix_span, KV_HEADS, HD), kv_ids, axis=2)
    suf_values = jnp.take(
        suffix_values.reshape(row_count, suffix_span, KV_HEADS, HD), kv_ids, axis=2
    )
    suf_scores = (
        jnp.einsum("rsd,rjsd->rsj", queries, suf_keys, preferred_element_type=jnp.float32)
        * score_scale
    )
    suf_live = (jnp.arange(suffix_span, dtype=jnp.int32)[None, :] < own_suffix[:, None])[:, None, :]
    suf_top = jnp.max(jnp.where(suf_live, suf_scores, NEG_FILL), axis=2)
    own_keys = jnp.take(new_keys, kv_ids, axis=1).astype(jnp.float32)
    own_values = jnp.take(new_values, kv_ids, axis=1).astype(jnp.float32)
    own_score = jnp.sum(queries.astype(jnp.float32) * own_keys, axis=-1) * score_scale
    final_top = jnp.maximum(jnp.maximum(part_top, suf_top), own_score)
    carried = jnp.exp(part_top - final_top)
    suf_weights = jnp.where(suf_live, jnp.exp(suf_scores - final_top[:, :, None]), 0.0)
    own_weight = jnp.exp(own_score - final_top)
    denominator = carried * part_total + jnp.sum(suf_weights, axis=2) + own_weight
    own_low = lax.optimization_barrier(own_weight.astype(jnp.bfloat16)).astype(jnp.float32)
    numerator = carried[..., None] * part_mixed + own_low[..., None] * own_values
    numerator = numerator + jnp.einsum(
        "rsj,rjsd->rsd",
        suf_weights.astype(jnp.bfloat16),
        suf_values,
        preferred_element_type=jnp.float32,
    )
    attended = (numerator / denominator[..., None] * slot_used[None, :, None]).astype(jnp.bfloat16)
    head_part = jnp.dot(
        attended.reshape(row_count, slot_count * HD), w_out, preferred_element_type=jnp.float32
    )
    head_total = tp_sum(head_part)
    hidden = (tokens.astype(jnp.float32) + head_total).astype(jnp.bfloat16)
    mlp_in = rms_scale(hidden, mlp_gain)
    gate_part = jnp.dot(mlp_in, w_gate, preferred_element_type=jnp.float32)
    up_part = jnp.dot(mlp_in, w_up, preferred_element_type=jnp.float32)
    activation = (jax.nn.silu(gate_part) * up_part).astype(jnp.bfloat16)
    down_part = jnp.dot(activation, w_down, preferred_element_type=jnp.float32)
    down_total = tp_sum(down_part)
    return (hidden.astype(jnp.float32) + down_total).astype(jnp.bfloat16)


def solution(mesh):
    return jax.shard_map(
        on_device,
        mesh=mesh,
        in_specs=(
            P("seq", None),
            P(),
            P(None, "tp"),
            P(),
            P(),
            P("tp", None),
            P(None, "seq", None),
            P(None, "seq", None),
            P("seq", None, None),
            P("seq", None, None),
            P(),
            P(),
            P(),
            P(),
            P(None, "tp"),
            P(None, "tp"),
            P("tp", None),
        ),
        out_specs=P("seq", None),
        check_vma=False,
    )
```

```python
import jax
import jax.numpy as jnp
from jax import lax
from jax.experimental import pallas as pl
from jax.experimental.pallas import tpu as pltpu
from jax.sharding import PartitionSpec as P

HEADS = 18
KV_HEADS = 6
HD = 64


NEG_FILL = -1e30
TILE = 64


def split_parts(values, count):
    parts = []
    for _ in range(count - 1):
        high = values.astype(jnp.bfloat16).astype(jnp.float32)
        parts.append(high)
        values = values - high
    parts.append(values.astype(jnp.bfloat16).astype(jnp.float32))
    return parts


def prefix_kernel(tile_of, group_at, valid, limit, kv, perm_ref, sg_ref, q_ref, k_ref, v_ref, o_ref):
    step = pl.program_id(0)
    tile = tile_of[step]
    first = jnp.logical_or(step == 0, tile_of[jnp.maximum(step - 1, 0)] != tile)
    rows, width = o_ref.shape
    lanes = 128
    slot_count = kv.shape[0]
    tail_at = (slot_count // 2) * lanes
    wide_lane = lax.broadcasted_iota(jnp.int32, (rows, width), 1)

    @pl.when(first)
    def _():
        top_lanes = jnp.logical_and(wide_lane >= tail_at + HD, wide_lane < tail_at + HD + slot_count)
        o_ref[...] = jnp.where(top_lanes, NEG_FILL, 0.0).astype(jnp.float32)

    group = group_at[step]
    live_count = limit[group]

    @pl.when(jnp.logical_and(valid[step] == 1, live_count > 0))
    def _():
        request_count = q_ref.shape[0]
        pick = (perm_ref[...] == lax.broadcasted_iota(jnp.int32, (rows, request_count), 1)).astype(jnp.bfloat16)
        q_rows = jnp.dot(pick, q_ref[...], preferred_element_type=jnp.float32)
        row_live = sg_ref[...] == group
        lane = lax.broadcasted_iota(jnp.int32, (rows, lanes), 1)
        upper = lane >= HD
        tile_total = width // lanes
        padded = []
        for slot in range(slot_count):
            head = kv[slot]
            odd = head % 2 == 1
            half = slot % 2 == 1
            block = q_rows[:, (slot // 2) * lanes : (slot // 2 + 1) * lanes]
            block = jnp.where(upper == half, block, 0.0)
            block = jnp.where(odd == half, block, pltpu.roll(block, HD, 1))
            padded.append(
                jnp.concatenate(
                    [jnp.where(head // 2 == j, block, 0.0) for j in range(tile_total)], axis=1
                ).astype(jnp.bfloat16)
            )
        padded = jnp.concatenate(padded, axis=0)
        scores = lax.dot_general(
            padded, k_ref[0], (((1,), (1,)), ((), ())), preferred_element_type=jnp.float32
        ) * (HD ** (-0.5))
        all_live = jnp.concatenate([row_live] * slot_count, axis=0)
        spots = lax.broadcasted_iota(jnp.int32, scores.shape, 1)
        live = jnp.logical_and(spots < live_count, all_live)
        top = jnp.max(jnp.where(live, scores, NEG_FILL), axis=1, keepdims=True)
        weights = jnp.where(live, jnp.exp(scores - top), 0.0)
        total = jnp.sum(weights, axis=1, keepdims=True)
        mixed = jnp.dot(weights.astype(jnp.bfloat16), v_ref[0], preferred_element_type=jnp.float32)
        pieces = []
        for slot in range(slot_count):
            head = kv[slot]
            odd = head % 2 == 1
            half = slot % 2 == 1
            mine = mixed[slot * rows : (slot + 1) * rows]
            chosen = mine[:, 0:lanes]
            for j in range(1, tile_total):
                chosen = jnp.where(head // 2 == j, mine[:, j * lanes : (j + 1) * lanes], chosen)
            pieces.append(jnp.where(odd == half, chosen, pltpu.roll(chosen, HD, 1)))
        if slot_count % 2:
            pieces.append(jnp.zeros((rows, lanes), jnp.float32))
        out = [jnp.where(upper, pieces[i + 1], pieces[i]) for i in range(0, len(pieces), 2)]
        tail = out[-1]
        parts = split_parts(top, 3) + split_parts(total, 3)
        for index, part in enumerate(parts):
            for slot in range(slot_count):
                tail = jnp.where(lane == HD + index * slot_count + slot, part[slot * rows : (slot + 1) * rows], tail)
        out[-1] = tail
        o_ref[...] = jnp.where(row_live, jnp.concatenate(out, axis=1), o_ref[...])


def prefix_partials(every_query, group_of, prefix_len, seq_index, prefix_keys, prefix_values, kv_ids):
    request_count, width = every_query.shape
    group_count, prefix_span, _ = prefix_keys.shape
    tile_count = request_count // TILE
    visit_count = tile_count + group_count - 1
    order_key = group_of * request_count + jnp.arange(request_count, dtype=jnp.int32)
    rank = jnp.sum((order_key[None, :] < order_key[:, None]).astype(jnp.int32), axis=1)
    spots = jnp.arange(request_count, dtype=jnp.int32)
    match = rank[None, :] == spots[:, None]
    perm = jnp.sum(jnp.where(match, spots[None, :], 0), axis=1)
    sorted_groups = jnp.sum(jnp.where(match, group_of[None, :], 0), axis=1)
    low = sorted_groups[0::TILE]
    high = sorted_groups[TILE - 1 :: TILE]
    spans = high - low + 1
    ends = jnp.cumsum(spans)
    starts = ends - spans
    visits = jnp.arange(visit_count, dtype=jnp.int32)
    tile_of = jnp.minimum(jnp.sum((ends[None, :] <= visits[:, None]).astype(jnp.int32), axis=1), tile_count - 1)
    valid = (visits < ends[-1]).astype(jnp.int32)
    group_at = jnp.where(valid == 1, jnp.take(low, tile_of) + visits - jnp.take(starts, tile_of), high[-1])
    limit = jnp.clip(prefix_len - seq_index * prefix_span, 0, prefix_span).astype(jnp.int32)
    slot_count = kv_ids.shape[0]
    grid_spec = pltpu.PrefetchScalarGridSpec(
        num_scalar_prefetch=5,
        grid=(visit_count,),
        in_specs=[
            pl.BlockSpec((TILE, 1), lambda i, t, g, ok, lim, kv: (t[i], 0)),
            pl.BlockSpec((TILE, 1), lambda i, t, g, ok, lim, kv: (t[i], 0)),
            pl.BlockSpec((request_count, width), lambda i, t, g, ok, lim, kv: (0, 0)),
            pl.BlockSpec((1, prefix_span, width), lambda i, t, g, ok, lim, kv: (g[i], 0, 0)),
            pl.BlockSpec((1, prefix_span, width), lambda i, t, g, ok, lim, kv: (g[i], 0, 0)),
        ],
        out_specs=pl.BlockSpec((TILE, width), lambda i, t, g, ok, lim, kv: (t[i], 0)),
    )
    lanes = 128
    flops = visit_count * (2 * TILE * request_count * width + slot_count * 4 * TILE * width * prefix_span)
    out = pl.pallas_call(
        prefix_kernel,
        grid_spec=grid_spec,
        out_shape=jax.ShapeDtypeStruct((request_count, width), jnp.float32),
        compiler_params=pltpu.CompilerParams(dimension_semantics=("arbitrary",)),
        cost_estimate=pl.CostEstimate(
            flops=flops,
            transcendentals=visit_count * TILE * slot_count * prefix_span,
            bytes_accessed=visit_count * 2 * prefix_span * width * 2 + request_count * width * 6,
        ),
    )(
        tile_of,
        group_at,
        valid,
        limit,
        kv_ids,
        perm.reshape(-1, 1),
        sorted_groups.reshape(-1, 1),
        every_query,
        prefix_keys,
        prefix_values,
    )
    return jnp.take(out, rank, axis=0).astype(jnp.bfloat16)


def rms_scale(values_in, gain_row):
    widened = values_in.astype(jnp.float32)
    factor = lax.rsqrt(jnp.mean(widened * widened, axis=-1, keepdims=True) + 1e-05)
    return (widened * factor * gain_row).astype(jnp.bfloat16)


def rotate_heads(blocks, position):
    half_dim = blocks.shape[-1] // 2
    frequency = jnp.power(10000.0, -jnp.arange(half_dim, dtype=jnp.float32) / half_dim)
    angles = position.astype(jnp.float32)[:, None, None] * frequency
    cosine = jnp.cos(angles)
    sine_part = jnp.sin(angles)
    low_half = blocks[..., :half_dim]
    high_half = blocks[..., half_dim:]
    return jnp.concatenate(
        [low_half * cosine - high_half * sine_part, high_half * cosine + low_half * sine_part],
        axis=-1,
    )


def slot_layout(device_tp, tp_count, slot_count):
    per_device = HEADS // tp_count
    surplus = HEADS % tp_count
    start_head = per_device * device_tp + jnp.minimum(device_tp, surplus)
    used_count = per_device + (device_tp < surplus).astype(jnp.int32)
    slot_ids = jnp.arange(slot_count, dtype=jnp.int32)
    head_ids = start_head + slot_ids
    slot_used = (slot_ids < used_count).astype(jnp.float32)
    kv_ids = jnp.minimum(head_ids, HEADS - 1) // (HEADS // KV_HEADS)
    return (kv_ids, slot_used)


def tp_sum(part):
    sent = part.astype(jnp.bfloat16)
    count = lax.axis_size("tp")
    total = sent.astype(jnp.float32)
    for shift in range(1, count):
        moved = lax.ppermute(sent, "tp", [(j, (j + shift) % count) for j in range(count)])
        total = total + moved.astype(jnp.float32)
    return total


def on_device(
    tokens,
    attn_gain,
    w_query,
    w_key,
    w_value,
    w_out,
    prefix_keys,
    prefix_values,
    suffix_keys,
    suffix_values,
    group_of,
    prefix_len,
    suffix_len,
    mlp_gain,
    w_gate,
    w_up,
    w_down,
):
    row_count = tokens.shape[0]
    slot_count = w_query.shape[1] // HD
    group_count = prefix_keys.shape[0]
    prefix_span = prefix_keys.shape[1]
    suffix_span = suffix_keys.shape[1]
    seq_index = lax.axis_index("seq")
    kv_ids, slot_used = slot_layout(lax.axis_index("tp"), lax.axis_size("tp"), slot_count)
    normed = rms_scale(tokens, attn_gain)
    queries = jnp.dot(normed, w_query, preferred_element_type=jnp.float32).reshape(
        row_count, slot_count, HD
    )
    new_keys = jnp.dot(normed, w_key, preferred_element_type=jnp.float32).reshape(
        row_count, KV_HEADS, HD
    )
    new_values = (
        jnp.dot(normed, w_value, preferred_element_type=jnp.float32)
        .astype(jnp.bfloat16)
        .reshape(row_count, KV_HEADS, HD)
    )
    own_start = seq_index * row_count
    own_groups = lax.dynamic_slice_in_dim(group_of, own_start, row_count)
    own_suffix = lax.dynamic_slice_in_dim(suffix_len, own_start, row_count)
    group_ids = jnp.arange(group_count, dtype=jnp.int32)
    own_prefix = jnp.sum(
        jnp.where(own_groups[:, None] == group_ids[None, :], prefix_len[None, :], 0), axis=1
    )
    position = own_prefix + own_suffix
    queries = rotate_heads(queries, position).astype(jnp.bfloat16)
    new_keys = rotate_heads(new_keys, position).astype(jnp.bfloat16)
    seq_count = lax.axis_size("seq")
    query_width = prefix_keys.shape[2]
    own_query = jnp.pad(
        queries.reshape(1, row_count, slot_count * HD),
        ((0, 0), (0, 0), (0, query_width - slot_count * HD)),
    )
    every_query = lax.all_to_all(
        jnp.broadcast_to(own_query, (seq_count, row_count, query_width)),
        "seq",
        0,
        0,
        tiled=True,
    )
    every_query = every_query.reshape(-1, query_width)
    score_scale = HD ** (-0.5)
    payload = prefix_partials(
        every_query, group_of, prefix_len, seq_index, prefix_keys, prefix_values, kv_ids
    )
    payload = payload.reshape(seq_count, row_count, query_width)
    gathered = lax.all_to_all(payload, "seq", 0, 0, tiled=True).astype(jnp.float32)
    tail_at = (slot_count // 2) * 128 + HD
    tail_parts = [gathered[..., tail_at + i * slot_count : tail_at + (i + 1) * slot_count] for i in range(6)]
    gathered_top = (tail_parts[0] + tail_parts[1]) + tail_parts[2]
    gathered_total = (tail_parts[3] + tail_parts[4]) + tail_parts[5]
    gathered_mixed = gathered[..., : slot_count * HD].reshape(seq_count, row_count, slot_count, HD)
    part_top = jnp.max(gathered_top, axis=0)
    part_scale = jnp.exp(gathered_top - part_top[None])
    part_total = jnp.sum(part_scale * gathered_total, axis=0)
    part_mixed = jnp.sum(part_scale[..., None] * gathered_mixed, axis=0)
    suf_keys = jnp.take(suffix_keys.reshape(row_count, suffix_span, KV_HEADS, HD), kv_ids, axis=2)
    suf_values = jnp.take(
        suffix_values.reshape(row_count, suffix_span, KV_HEADS, HD), kv_ids, axis=2
    )
    suf_scores = (
        jnp.einsum("rsd,rjsd->rsj", queries, suf_keys, preferred_element_type=jnp.float32)
        * score_scale
    )
    suf_live = (jnp.arange(suffix_span, dtype=jnp.int32)[None, :] < own_suffix[:, None])[:, None, :]
    suf_top = jnp.max(jnp.where(suf_live, suf_scores, NEG_FILL), axis=2)
    own_keys = jnp.take(new_keys, kv_ids, axis=1).astype(jnp.float32)
    own_values = jnp.take(new_values, kv_ids, axis=1).astype(jnp.float32)
    own_score = jnp.sum(queries.astype(jnp.float32) * own_keys, axis=-1) * score_scale
    local_top = jnp.maximum(suf_top, own_score)
    suf_weights = jnp.where(suf_live, jnp.exp(suf_scores - local_top[:, :, None]), 0.0)
    own_weight = jnp.exp(own_score - local_top)
    local_total = jnp.sum(suf_weights, axis=2) + own_weight
    own_low = lax.optimization_barrier(own_weight.astype(jnp.bfloat16)).astype(jnp.float32)
    local_mixed = own_low[..., None] * own_values + jnp.einsum(
        "rsj,rjsd->rsd",
        suf_weights.astype(jnp.bfloat16),
        suf_values,
        preferred_element_type=jnp.float32,
    )
    final_top = jnp.maximum(part_top, local_top)
    carried = jnp.exp(part_top - final_top)
    kept = jnp.exp(local_top - final_top)
    denominator = carried * part_total + kept * local_total
    numerator = carried[..., None] * part_mixed + kept[..., None] * local_mixed
    attended = (numerator / denominator[..., None] * slot_used[None, :, None]).astype(jnp.bfloat16)
    head_part = jnp.dot(
        attended.reshape(row_count, slot_count * HD), w_out, preferred_element_type=jnp.float32
    )
    head_total = tp_sum(head_part)
    hidden = (tokens.astype(jnp.float32) + head_total).astype(jnp.bfloat16)
    mlp_in = rms_scale(hidden, mlp_gain)
    gate_part = jnp.dot(mlp_in, w_gate, preferred_element_type=jnp.float32)
    up_part = jnp.dot(mlp_in, w_up, preferred_element_type=jnp.float32)
    activation = (jax.nn.silu(gate_part) * up_part).astype(jnp.bfloat16)
    down_part = jnp.dot(activation, w_down, preferred_element_type=jnp.float32)
    down_total = tp_sum(down_part)
    return (hidden.astype(jnp.float32) + down_total).astype(jnp.bfloat16)


def solution(mesh):
    return jax.shard_map(
        on_device,
        mesh=mesh,
        in_specs=(
            P("seq", None),
            P(),
            P(None, "tp"),
            P(),
            P(),
            P("tp", None),
            P(None, "seq", None),
            P(None, "seq", None),
            P("seq", None, None),
            P("seq", None, None),
            P(),
            P(),
            P(),
            P(),
            P(None, "tp"),
            P(None, "tp"),
            P("tp", None),
        ),
        out_specs=P("seq", None),
        check_vma=False,
    )
```

```python
import jax
import jax.numpy as jnp
from jax import lax
from jax.experimental import pallas as pl
from jax.experimental.pallas import tpu as pltpu
from jax.sharding import PartitionSpec as P

HEADS = 18
KV_HEADS = 6
HD = 64


NEG_FILL = -1e30
TILE = 64


def split_parts(values, count):
    parts = []
    for _ in range(count - 1):
        high = values.astype(jnp.bfloat16).astype(jnp.float32)
        parts.append(high)
        values = values - high
    parts.append(values.astype(jnp.bfloat16).astype(jnp.float32))
    return parts


def prefix_kernel(tile_of, group_at, valid, limit, kv, perm_ref, sg_ref, q_ref, k_ref, v_ref, o_ref):
    step = pl.program_id(0)
    tile = tile_of[step]
    first = jnp.logical_or(step == 0, tile_of[jnp.maximum(step - 1, 0)] != tile)
    rows, width = o_ref.shape
    lanes = 128
    slot_count = kv.shape[0]
    tail_at = (slot_count // 2) * lanes
    wide_lane = lax.broadcasted_iota(jnp.int32, (rows, width), 1)

    @pl.when(first)
    def _():
        top_lanes = jnp.logical_and(wide_lane >= tail_at + HD, wide_lane < tail_at + HD + slot_count)
        o_ref[...] = jnp.where(top_lanes, NEG_FILL, 0.0).astype(o_ref.dtype)

    group = group_at[step]
    live_count = limit[group]

    @pl.when(jnp.logical_and(valid[step] == 1, live_count > 0))
    def _():
        request_count = q_ref.shape[0]
        pick = (perm_ref[...] == lax.broadcasted_iota(jnp.int32, (rows, request_count), 1)).astype(jnp.bfloat16)
        q_rows = jnp.dot(pick, q_ref[...], preferred_element_type=jnp.float32)
        row_live = sg_ref[...] == group
        lane = lax.broadcasted_iota(jnp.int32, (rows, lanes), 1)
        upper = lane >= HD
        tile_total = width // lanes
        padded = []
        for slot in range(slot_count):
            head = kv[slot]
            odd = head % 2 == 1
            half = slot % 2 == 1
            block = q_rows[:, (slot // 2) * lanes : (slot // 2 + 1) * lanes]
            block = jnp.where(upper == half, block, 0.0)
            block = jnp.where(odd == half, block, pltpu.roll(block, HD, 1))
            padded.append(
                jnp.concatenate(
                    [jnp.where(head // 2 == j, block, 0.0) for j in range(tile_total)], axis=1
                ).astype(jnp.bfloat16)
            )
        padded = jnp.concatenate(padded, axis=0)
        scores = lax.dot_general(
            padded, k_ref[0], (((1,), (1,)), ((), ())), preferred_element_type=jnp.float32
        ) * (HD ** (-0.5))
        all_live = jnp.concatenate([row_live] * slot_count, axis=0)
        spots = lax.broadcasted_iota(jnp.int32, scores.shape, 1)
        live = jnp.logical_and(spots < live_count, all_live)
        top = jnp.max(jnp.where(live, scores, NEG_FILL), axis=1, keepdims=True)
        weights = jnp.where(live, jnp.exp(scores - top), 0.0)
        total = jnp.sum(weights, axis=1, keepdims=True)
        mixed = jnp.dot(weights.astype(jnp.bfloat16), v_ref[0], preferred_element_type=jnp.float32)
        pieces = []
        for slot in range(slot_count):
            head = kv[slot]
            odd = head % 2 == 1
            half = slot % 2 == 1
            mine = mixed[slot * rows : (slot + 1) * rows]
            chosen = mine[:, 0:lanes]
            for j in range(1, tile_total):
                chosen = jnp.where(head // 2 == j, mine[:, j * lanes : (j + 1) * lanes], chosen)
            pieces.append(jnp.where(odd == half, chosen, pltpu.roll(chosen, HD, 1)))
        if slot_count % 2:
            pieces.append(jnp.zeros((rows, lanes), jnp.float32))
        out = [jnp.where(upper, pieces[i + 1], pieces[i]) for i in range(0, len(pieces), 2)]
        tail = out[-1]
        parts = split_parts(top, 3) + split_parts(total, 3)
        for index, part in enumerate(parts):
            for slot in range(slot_count):
                tail = jnp.where(lane == HD + index * slot_count + slot, part[slot * rows : (slot + 1) * rows], tail)
        out[-1] = tail
        o_ref[...] = jnp.where(row_live, jnp.concatenate(out, axis=1).astype(o_ref.dtype), o_ref[...])


def prefix_partials(every_query, group_of, prefix_len, seq_index, prefix_keys, prefix_values, kv_ids):
    request_count, width = every_query.shape
    group_count, prefix_span, _ = prefix_keys.shape
    tile_count = request_count // TILE
    visit_count = tile_count + group_count - 1
    order_key = group_of * request_count + jnp.arange(request_count, dtype=jnp.int32)
    rank = jnp.sum((order_key[None, :] < order_key[:, None]).astype(jnp.int32), axis=1)
    spots = jnp.arange(request_count, dtype=jnp.int32)
    match = rank[None, :] == spots[:, None]
    perm = jnp.sum(jnp.where(match, spots[None, :], 0), axis=1)
    sorted_groups = jnp.sum(jnp.where(match, group_of[None, :], 0), axis=1)
    low = sorted_groups[0::TILE]
    high = sorted_groups[TILE - 1 :: TILE]
    spans = high - low + 1
    ends = jnp.cumsum(spans)
    starts = ends - spans
    visits = jnp.arange(visit_count, dtype=jnp.int32)
    tile_of = jnp.minimum(jnp.sum((ends[None, :] <= visits[:, None]).astype(jnp.int32), axis=1), tile_count - 1)
    valid = (visits < ends[-1]).astype(jnp.int32)
    group_at = jnp.where(valid == 1, jnp.take(low, tile_of) + visits - jnp.take(starts, tile_of), high[-1])
    limit = jnp.clip(prefix_len - seq_index * prefix_span, 0, prefix_span).astype(jnp.int32)
    slot_count = kv_ids.shape[0]
    grid_spec = pltpu.PrefetchScalarGridSpec(
        num_scalar_prefetch=5,
        grid=(visit_count,),
        in_specs=[
            pl.BlockSpec((TILE, 1), lambda i, t, g, ok, lim, kv: (t[i], 0)),
            pl.BlockSpec((TILE, 1), lambda i, t, g, ok, lim, kv: (t[i], 0)),
            pl.BlockSpec((request_count, width), lambda i, t, g, ok, lim, kv: (0, 0)),
            pl.BlockSpec((1, prefix_span, width), lambda i, t, g, ok, lim, kv: (g[i], 0, 0)),
            pl.BlockSpec((1, prefix_span, width), lambda i, t, g, ok, lim, kv: (g[i], 0, 0)),
        ],
        out_specs=pl.BlockSpec((TILE, width), lambda i, t, g, ok, lim, kv: (t[i], 0)),
    )
    lanes = 128
    flops = visit_count * (2 * TILE * request_count * width + slot_count * 4 * TILE * width * prefix_span)
    out = pl.pallas_call(
        prefix_kernel,
        grid_spec=grid_spec,
        out_shape=jax.ShapeDtypeStruct((request_count, width), jnp.bfloat16),
        compiler_params=pltpu.CompilerParams(dimension_semantics=("arbitrary",)),
        cost_estimate=pl.CostEstimate(
            flops=flops,
            transcendentals=visit_count * TILE * slot_count * prefix_span,
            bytes_accessed=visit_count * 2 * prefix_span * width * 2 + request_count * width * 6,
        ),
    )(
        tile_of,
        group_at,
        valid,
        limit,
        kv_ids,
        perm.reshape(-1, 1),
        sorted_groups.reshape(-1, 1),
        every_query,
        prefix_keys,
        prefix_values,
    )
    unsort = (rank[:, None] == spots[None, :]).astype(jnp.bfloat16)
    return jnp.dot(unsort, out, preferred_element_type=jnp.float32).astype(jnp.bfloat16)


def rms_scale(values_in, gain_row):
    widened = values_in.astype(jnp.float32)
    factor = lax.rsqrt(jnp.mean(widened * widened, axis=-1, keepdims=True) + 1e-05)
    return (widened * factor * gain_row).astype(jnp.bfloat16)


def rotate_heads(blocks, position):
    half_dim = blocks.shape[-1] // 2
    frequency = jnp.power(10000.0, -jnp.arange(half_dim, dtype=jnp.float32) / half_dim)
    angles = position.astype(jnp.float32)[:, None, None] * frequency
    cosine = jnp.cos(angles)
    sine_part = jnp.sin(angles)
    low_half = blocks[..., :half_dim]
    high_half = blocks[..., half_dim:]
    return jnp.concatenate(
        [low_half * cosine - high_half * sine_part, high_half * cosine + low_half * sine_part],
        axis=-1,
    )


def slot_layout(device_tp, tp_count, slot_count):
    per_device = HEADS // tp_count
    surplus = HEADS % tp_count
    start_head = per_device * device_tp + jnp.minimum(device_tp, surplus)
    used_count = per_device + (device_tp < surplus).astype(jnp.int32)
    slot_ids = jnp.arange(slot_count, dtype=jnp.int32)
    head_ids = start_head + slot_ids
    slot_used = (slot_ids < used_count).astype(jnp.float32)
    kv_ids = jnp.minimum(head_ids, HEADS - 1) // (HEADS // KV_HEADS)
    return (kv_ids, slot_used)


def tp_sum(part):
    sent = part.astype(jnp.bfloat16)
    count = lax.axis_size("tp")
    total = sent.astype(jnp.float32)
    for shift in range(1, count):
        moved = lax.ppermute(sent, "tp", [(j, (j + shift) % count) for j in range(count)])
        total = total + moved.astype(jnp.float32)
    return total


def on_device(
    tokens,
    attn_gain,
    w_query,
    w_key,
    w_value,
    w_out,
    prefix_keys,
    prefix_values,
    suffix_keys,
    suffix_values,
    group_of,
    prefix_len,
    suffix_len,
    mlp_gain,
    w_gate,
    w_up,
    w_down,
):
    row_count = tokens.shape[0]
    slot_count = w_query.shape[1] // HD
    group_count = prefix_keys.shape[0]
    prefix_span = prefix_keys.shape[1]
    suffix_span = suffix_keys.shape[1]
    seq_index = lax.axis_index("seq")
    kv_ids, slot_used = slot_layout(lax.axis_index("tp"), lax.axis_size("tp"), slot_count)
    normed = rms_scale(tokens, attn_gain)
    queries = jnp.dot(normed, w_query, preferred_element_type=jnp.float32).reshape(
        row_count, slot_count, HD
    )
    new_keys = jnp.dot(normed, w_key, preferred_element_type=jnp.float32).reshape(
        row_count, KV_HEADS, HD
    )
    new_values = (
        jnp.dot(normed, w_value, preferred_element_type=jnp.float32)
        .astype(jnp.bfloat16)
        .reshape(row_count, KV_HEADS, HD)
    )
    own_start = seq_index * row_count
    own_groups = lax.dynamic_slice_in_dim(group_of, own_start, row_count)
    own_suffix = lax.dynamic_slice_in_dim(suffix_len, own_start, row_count)
    group_ids = jnp.arange(group_count, dtype=jnp.int32)
    own_prefix = jnp.sum(
        jnp.where(own_groups[:, None] == group_ids[None, :], prefix_len[None, :], 0), axis=1
    )
    position = own_prefix + own_suffix
    queries = rotate_heads(queries, position).astype(jnp.bfloat16)
    new_keys = rotate_heads(new_keys, position).astype(jnp.bfloat16)
    seq_count = lax.axis_size("seq")
    query_width = prefix_keys.shape[2]
    own_query = jnp.pad(
        queries.reshape(1, row_count, slot_count * HD),
        ((0, 0), (0, 0), (0, query_width - slot_count * HD)),
    )
    every_query = lax.all_to_all(
        jnp.broadcast_to(own_query, (seq_count, row_count, query_width)),
        "seq",
        0,
        0,
        tiled=True,
    )
    every_query = every_query.reshape(-1, query_width)
    score_scale = HD ** (-0.5)
    payload = prefix_partials(
        every_query, group_of, prefix_len, seq_index, prefix_keys, prefix_values, kv_ids
    )
    payload = payload.reshape(seq_count, row_count, query_width)
    gathered = lax.all_to_all(payload, "seq", 0, 0, tiled=True).astype(jnp.float32)
    tail_at = (slot_count // 2) * 128 + HD
    tail_parts = [gathered[..., tail_at + i * slot_count : tail_at + (i + 1) * slot_count] for i in range(6)]
    gathered_top = (tail_parts[0] + tail_parts[1]) + tail_parts[2]
    gathered_total = (tail_parts[3] + tail_parts[4]) + tail_parts[5]
    gathered_mixed = gathered[..., : slot_count * HD].reshape(seq_count, row_count, slot_count, HD)
    part_top = jnp.max(gathered_top, axis=0)
    part_scale = jnp.exp(gathered_top - part_top[None])
    part_total = jnp.sum(part_scale * gathered_total, axis=0)
    part_mixed = jnp.sum(part_scale[..., None] * gathered_mixed, axis=0)
    suf_keys = jnp.take(suffix_keys.reshape(row_count, suffix_span, KV_HEADS, HD), kv_ids, axis=2)
    suf_values = jnp.take(
        suffix_values.reshape(row_count, suffix_span, KV_HEADS, HD), kv_ids, axis=2
    )
    suf_scores = (
        jnp.einsum("rsd,rjsd->rsj", queries, suf_keys, preferred_element_type=jnp.float32)
        * score_scale
    )
    suf_live = (jnp.arange(suffix_span, dtype=jnp.int32)[None, :] < own_suffix[:, None])[:, None, :]
    suf_top = jnp.max(jnp.where(suf_live, suf_scores, NEG_FILL), axis=2)
    own_keys = jnp.take(new_keys, kv_ids, axis=1).astype(jnp.float32)
    own_values = jnp.take(new_values, kv_ids, axis=1).astype(jnp.float32)
    own_score = jnp.sum(queries.astype(jnp.float32) * own_keys, axis=-1) * score_scale
    local_top = jnp.maximum(suf_top, own_score)
    suf_weights = jnp.where(suf_live, jnp.exp(suf_scores - local_top[:, :, None]), 0.0)
    own_weight = jnp.exp(own_score - local_top)
    local_total = jnp.sum(suf_weights, axis=2) + own_weight
    own_low = lax.optimization_barrier(own_weight.astype(jnp.bfloat16)).astype(jnp.float32)
    local_mixed = own_low[..., None] * own_values + jnp.einsum(
        "rsj,rjsd->rsd",
        suf_weights.astype(jnp.bfloat16),
        suf_values,
        preferred_element_type=jnp.float32,
    )
    final_top = jnp.maximum(part_top, local_top)
    carried = jnp.exp(part_top - final_top)
    kept = jnp.exp(local_top - final_top)
    denominator = carried * part_total + kept * local_total
    numerator = carried[..., None] * part_mixed + kept[..., None] * local_mixed
    attended = (numerator / denominator[..., None] * slot_used[None, :, None]).astype(jnp.bfloat16)
    head_part = jnp.dot(
        attended.reshape(row_count, slot_count * HD), w_out, preferred_element_type=jnp.float32
    )
    head_total = tp_sum(head_part)
    hidden = (tokens.astype(jnp.float32) + head_total).astype(jnp.bfloat16)
    mlp_in = rms_scale(hidden, mlp_gain)
    gate_part = jnp.dot(mlp_in, w_gate, preferred_element_type=jnp.float32)
    up_part = jnp.dot(mlp_in, w_up, preferred_element_type=jnp.float32)
    activation = (jax.nn.silu(gate_part) * up_part).astype(jnp.bfloat16)
    down_part = jnp.dot(activation, w_down, preferred_element_type=jnp.float32)
    down_total = tp_sum(down_part)
    return (hidden.astype(jnp.float32) + down_total).astype(jnp.bfloat16)


def solution(mesh):
    return jax.shard_map(
        on_device,
        mesh=mesh,
        in_specs=(
            P("seq", None),
            P(),
            P(None, "tp"),
            P(),
            P(),
            P("tp", None),
            P(None, "seq", None),
            P(None, "seq", None),
            P("seq", None, None),
            P("seq", None, None),
            P(),
            P(),
            P(),
            P(),
            P(None, "tp"),
            P(None, "tp"),
            P("tp", None),
        ),
        out_specs=P("seq", None),
        check_vma=False,
    )
```

```python
import functools

import jax
import numpy as np
import jax.numpy as jnp
from jax import lax
from jax.experimental import pallas as pl
from jax.experimental.pallas import tpu as pltpu
from jax.sharding import PartitionSpec as P

HEADS = 18
KV_HEADS = 6
HD = 64


NEG_FILL = -1e30
TILE = 64


def split_parts(values, count):
    parts = []
    for _ in range(count - 1):
        high = values.astype(jnp.bfloat16).astype(jnp.float32)
        parts.append(high)
        values = values - high
    parts.append(values.astype(jnp.bfloat16).astype(jnp.float32))
    return parts


def pair_window(tp_count, slot_count, width):
    spans = []
    for device_tp in range(tp_count):
        per_device = HEADS // tp_count
        start_head = per_device * device_tp + min(device_tp, HEADS % tp_count)
        heads = np.minimum(start_head + np.arange(slot_count), HEADS - 1) // (HEADS // KV_HEADS)
        spans.append(heads.max() // 2 - heads.min() // 2 + 1)
    return int(min(max(spans), width // 128))


def prefix_kernel(tile_of, group_at, valid, limit, kv, perm_ref, sg_ref, q_ref, k_ref, v_ref, o_ref, *, window):
    step = pl.program_id(0)
    tile = tile_of[step]
    first = jnp.logical_or(step == 0, tile_of[jnp.maximum(step - 1, 0)] != tile)
    rows, width = o_ref.shape
    lanes = 128
    slot_count = kv.shape[0]
    tail_at = (slot_count // 2) * lanes
    wide_lane = lax.broadcasted_iota(jnp.int32, (rows, width), 1)

    @pl.when(first)
    def _():
        top_lanes = jnp.logical_and(wide_lane >= tail_at + HD, wide_lane < tail_at + HD + slot_count)
        o_ref[...] = jnp.where(top_lanes, NEG_FILL, 0.0).astype(o_ref.dtype)

    group = group_at[step]
    live_count = limit[group]

    @pl.when(jnp.logical_and(valid[step] == 1, live_count > 0))
    def _():
        request_count = q_ref.shape[0]
        pick = (perm_ref[...] == lax.broadcasted_iota(jnp.int32, (rows, request_count), 1)).astype(jnp.bfloat16)
        q_rows = jnp.dot(pick, q_ref[...], preferred_element_type=jnp.float32)
        row_live = sg_ref[...] == group
        lane = lax.broadcasted_iota(jnp.int32, (rows, lanes), 1)
        upper = lane >= HD
        tile_total = window
        base = kv[0] // 2
        for slot in range(1, slot_count):
            base = jnp.minimum(base, kv[slot] // 2)
        base = jnp.minimum(base, width // lanes - window)
        start = pl.multiple_of(base * lanes, lanes)
        padded = []
        for slot in range(slot_count):
            head = kv[slot]
            odd = head % 2 == 1
            half = slot % 2 == 1
            block = q_rows[:, (slot // 2) * lanes : (slot // 2 + 1) * lanes]
            block = jnp.where(upper == half, block, 0.0)
            block = jnp.where(odd == half, block, pltpu.roll(block, HD, 1))
            padded.append(
                jnp.concatenate(
                    [jnp.where(head // 2 - base == j, block, 0.0) for j in range(tile_total)], axis=1
                ).astype(jnp.bfloat16)
            )
        padded = jnp.concatenate(padded, axis=0)
        scores = lax.dot_general(
            padded, k_ref[0, :, pl.ds(start, window * lanes)], (((1,), (1,)), ((), ())), preferred_element_type=jnp.float32
        ) * (HD ** (-0.5))
        all_live = jnp.concatenate([row_live] * slot_count, axis=0)
        spots = lax.broadcasted_iota(jnp.int32, scores.shape, 1)
        live = jnp.logical_and(spots < live_count, all_live)
        top = jnp.max(jnp.where(live, scores, NEG_FILL), axis=1, keepdims=True)
        weights = jnp.where(live, jnp.exp(scores - top), 0.0)
        total = jnp.sum(weights, axis=1, keepdims=True)
        mixed = jnp.dot(
            weights.astype(jnp.bfloat16), v_ref[0, :, pl.ds(start, window * lanes)], preferred_element_type=jnp.float32
        )
        pieces = []
        for slot in range(slot_count):
            head = kv[slot]
            odd = head % 2 == 1
            half = slot % 2 == 1
            mine = mixed[slot * rows : (slot + 1) * rows]
            chosen = mine[:, 0:lanes]
            for j in range(1, tile_total):
                chosen = jnp.where(head // 2 - base == j, mine[:, j * lanes : (j + 1) * lanes], chosen)
            pieces.append(jnp.where(odd == half, chosen, pltpu.roll(chosen, HD, 1)))
        if slot_count % 2:
            pieces.append(jnp.zeros((rows, lanes), jnp.float32))
        out = [jnp.where(upper, pieces[i + 1], pieces[i]) for i in range(0, len(pieces), 2)]
        tail = out[-1]
        parts = split_parts(top, 3) + split_parts(total, 3)
        for index, part in enumerate(parts):
            for slot in range(slot_count):
                tail = jnp.where(lane == HD + index * slot_count + slot, part[slot * rows : (slot + 1) * rows], tail)
        out[-1] = tail
        o_ref[...] = jnp.where(row_live, jnp.concatenate(out, axis=1).astype(o_ref.dtype), o_ref[...])


def prefix_partials(every_query, group_of, prefix_len, seq_index, prefix_keys, prefix_values, kv_ids, tp_count):
    request_count, width = every_query.shape
    group_count, prefix_span, _ = prefix_keys.shape
    tile_count = request_count // TILE
    visit_count = tile_count + group_count - 1
    order_key = group_of * request_count + jnp.arange(request_count, dtype=jnp.int32)
    rank = jnp.sum((order_key[None, :] < order_key[:, None]).astype(jnp.int32), axis=1)
    spots = jnp.arange(request_count, dtype=jnp.int32)
    match = rank[None, :] == spots[:, None]
    perm = jnp.sum(jnp.where(match, spots[None, :], 0), axis=1)
    sorted_groups = jnp.sum(jnp.where(match, group_of[None, :], 0), axis=1)
    low = sorted_groups[0::TILE]
    high = sorted_groups[TILE - 1 :: TILE]
    spans = high - low + 1
    ends = jnp.cumsum(spans)
    starts = ends - spans
    visits = jnp.arange(visit_count, dtype=jnp.int32)
    tile_of = jnp.minimum(jnp.sum((ends[None, :] <= visits[:, None]).astype(jnp.int32), axis=1), tile_count - 1)
    valid = (visits < ends[-1]).astype(jnp.int32)
    group_at = jnp.where(valid == 1, jnp.take(low, tile_of) + visits - jnp.take(starts, tile_of), high[-1])
    limit = jnp.clip(prefix_len - seq_index * prefix_span, 0, prefix_span).astype(jnp.int32)
    slot_count = kv_ids.shape[0]
    grid_spec = pltpu.PrefetchScalarGridSpec(
        num_scalar_prefetch=5,
        grid=(visit_count,),
        in_specs=[
            pl.BlockSpec((TILE, 1), lambda i, t, g, ok, lim, kv: (t[i], 0)),
            pl.BlockSpec((TILE, 1), lambda i, t, g, ok, lim, kv: (t[i], 0)),
            pl.BlockSpec((request_count, width), lambda i, t, g, ok, lim, kv: (0, 0)),
            pl.BlockSpec((1, prefix_span, width), lambda i, t, g, ok, lim, kv: (g[i], 0, 0)),
            pl.BlockSpec((1, prefix_span, width), lambda i, t, g, ok, lim, kv: (g[i], 0, 0)),
        ],
        out_specs=pl.BlockSpec((TILE, width), lambda i, t, g, ok, lim, kv: (t[i], 0)),
    )
    lanes = 128
    flops = visit_count * (2 * TILE * request_count * width + slot_count * 4 * TILE * width * prefix_span)
    window = pair_window(tp_count, slot_count, width)
    out = pl.pallas_call(
        functools.partial(prefix_kernel, window=window),
        grid_spec=grid_spec,
        out_shape=jax.ShapeDtypeStruct((request_count, width), jnp.bfloat16),
        compiler_params=pltpu.CompilerParams(dimension_semantics=("arbitrary",)),
        cost_estimate=pl.CostEstimate(
            flops=flops,
            transcendentals=visit_count * TILE * slot_count * prefix_span,
            bytes_accessed=visit_count * 2 * prefix_span * width * 2 + request_count * width * 6,
        ),
    )(
        tile_of,
        group_at,
        valid,
        limit,
        kv_ids,
        perm.reshape(-1, 1),
        sorted_groups.reshape(-1, 1),
        every_query,
        prefix_keys,
        prefix_values,
    )
    unsort = (rank[:, None] == spots[None, :]).astype(jnp.bfloat16)
    return jnp.dot(unsort, out, preferred_element_type=jnp.float32).astype(jnp.bfloat16)


def rms_scale(values_in, gain_row):
    widened = values_in.astype(jnp.float32)
    factor = lax.rsqrt(jnp.mean(widened * widened, axis=-1, keepdims=True) + 1e-05)
    return (widened * factor * gain_row).astype(jnp.bfloat16)


def rotate_heads(blocks, position):
    half_dim = blocks.shape[-1] // 2
    frequency = jnp.power(10000.0, -jnp.arange(half_dim, dtype=jnp.float32) / half_dim)
    angles = position.astype(jnp.float32)[:, None, None] * frequency
    cosine = jnp.cos(angles)
    sine_part = jnp.sin(angles)
    low_half = blocks[..., :half_dim]
    high_half = blocks[..., half_dim:]
    return jnp.concatenate(
        [low_half * cosine - high_half * sine_part, high_half * cosine + low_half * sine_part],
        axis=-1,
    )


def slot_layout(device_tp, tp_count, slot_count):
    per_device = HEADS // tp_count
    surplus = HEADS % tp_count
    start_head = per_device * device_tp + jnp.minimum(device_tp, surplus)
    used_count = per_device + (device_tp < surplus).astype(jnp.int32)
    slot_ids = jnp.arange(slot_count, dtype=jnp.int32)
    head_ids = start_head + slot_ids
    slot_used = (slot_ids < used_count).astype(jnp.float32)
    kv_ids = jnp.minimum(head_ids, HEADS - 1) // (HEADS // KV_HEADS)
    return (kv_ids, slot_used)


def tp_sum(part):
    sent = part.astype(jnp.bfloat16)
    count = lax.axis_size("tp")
    total = sent.astype(jnp.float32)
    for shift in range(1, count):
        moved = lax.ppermute(sent, "tp", [(j, (j + shift) % count) for j in range(count)])
        total = total + moved.astype(jnp.float32)
    return total


def on_device(
    tokens,
    attn_gain,
    w_query,
    w_key,
    w_value,
    w_out,
    prefix_keys,
    prefix_values,
    suffix_keys,
    suffix_values,
    group_of,
    prefix_len,
    suffix_len,
    mlp_gain,
    w_gate,
    w_up,
    w_down,
):
    row_count = tokens.shape[0]
    slot_count = w_query.shape[1] // HD
    group_count = prefix_keys.shape[0]
    prefix_span = prefix_keys.shape[1]
    suffix_span = suffix_keys.shape[1]
    seq_index = lax.axis_index("seq")
    kv_ids, slot_used = slot_layout(lax.axis_index("tp"), lax.axis_size("tp"), slot_count)
    normed = rms_scale(tokens, attn_gain)
    queries = jnp.dot(normed, w_query, preferred_element_type=jnp.float32).reshape(
        row_count, slot_count, HD
    )
    new_keys = jnp.dot(normed, w_key, preferred_element_type=jnp.float32).reshape(
        row_count, KV_HEADS, HD
    )
    new_values = (
        jnp.dot(normed, w_value, preferred_element_type=jnp.float32)
        .astype(jnp.bfloat16)
        .reshape(row_count, KV_HEADS, HD)
    )
    own_start = seq_index * row_count
    own_groups = lax.dynamic_slice_in_dim(group_of, own_start, row_count)
    own_suffix = lax.dynamic_slice_in_dim(suffix_len, own_start, row_count)
    group_ids = jnp.arange(group_count, dtype=jnp.int32)
    own_prefix = jnp.sum(
        jnp.where(own_groups[:, None] == group_ids[None, :], prefix_len[None, :], 0), axis=1
    )
    position = own_prefix + own_suffix
    queries = rotate_heads(queries, position).astype(jnp.bfloat16)
    new_keys = rotate_heads(new_keys, position).astype(jnp.bfloat16)
    seq_count = lax.axis_size("seq")
    query_width = prefix_keys.shape[2]
    own_query = jnp.pad(
        queries.reshape(1, row_count, slot_count * HD),
        ((0, 0), (0, 0), (0, query_width - slot_count * HD)),
    )
    every_query = lax.all_to_all(
        jnp.broadcast_to(own_query, (seq_count, row_count, query_width)),
        "seq",
        0,
        0,
        tiled=True,
    )
    every_query = every_query.reshape(-1, query_width)
    score_scale = HD ** (-0.5)
    payload = prefix_partials(
        every_query, group_of, prefix_len, seq_index, prefix_keys, prefix_values, kv_ids, lax.axis_size("tp")
    )
    payload = payload.reshape(seq_count, row_count, query_width)
    gathered = lax.all_to_all(payload, "seq", 0, 0, tiled=True).astype(jnp.float32)
    tail_at = (slot_count // 2) * 128 + HD
    tail_parts = [gathered[..., tail_at + i * slot_count : tail_at + (i + 1) * slot_count] for i in range(6)]
    gathered_top = (tail_parts[0] + tail_parts[1]) + tail_parts[2]
    gathered_total = (tail_parts[3] + tail_parts[4]) + tail_parts[5]
    gathered_mixed = gathered[..., : slot_count * HD].reshape(seq_count, row_count, slot_count, HD)
    part_top = jnp.max(gathered_top, axis=0)
    part_scale = jnp.exp(gathered_top - part_top[None])
    part_total = jnp.sum(part_scale * gathered_total, axis=0)
    part_mixed = jnp.sum(part_scale[..., None] * gathered_mixed, axis=0)
    suf_keys = jnp.take(suffix_keys.reshape(row_count, suffix_span, KV_HEADS, HD), kv_ids, axis=2)
    suf_values = jnp.take(
        suffix_values.reshape(row_count, suffix_span, KV_HEADS, HD), kv_ids, axis=2
    )
    suf_scores = (
        jnp.einsum("rsd,rjsd->rsj", queries, suf_keys, preferred_element_type=jnp.float32)
        * score_scale
    )
    suf_live = (jnp.arange(suffix_span, dtype=jnp.int32)[None, :] < own_suffix[:, None])[:, None, :]
    suf_top = jnp.max(jnp.where(suf_live, suf_scores, NEG_FILL), axis=2)
    own_keys = jnp.take(new_keys, kv_ids, axis=1).astype(jnp.float32)
    own_values = jnp.take(new_values, kv_ids, axis=1).astype(jnp.float32)
    own_score = jnp.sum(queries.astype(jnp.float32) * own_keys, axis=-1) * score_scale
    local_top = jnp.maximum(suf_top, own_score)
    suf_weights = jnp.where(suf_live, jnp.exp(suf_scores - local_top[:, :, None]), 0.0)
    own_weight = jnp.exp(own_score - local_top)
    local_total = jnp.sum(suf_weights, axis=2) + own_weight
    own_low = lax.optimization_barrier(own_weight.astype(jnp.bfloat16)).astype(jnp.float32)
    local_mixed = own_low[..., None] * own_values + jnp.einsum(
        "rsj,rjsd->rsd",
        suf_weights.astype(jnp.bfloat16),
        suf_values,
        preferred_element_type=jnp.float32,
    )
    final_top = jnp.maximum(part_top, local_top)
    carried = jnp.exp(part_top - final_top)
    kept = jnp.exp(local_top - final_top)
    denominator = carried * part_total + kept * local_total
    numerator = carried[..., None] * part_mixed + kept[..., None] * local_mixed
    attended = (numerator / denominator[..., None] * slot_used[None, :, None]).astype(jnp.bfloat16)
    head_part = jnp.dot(
        attended.reshape(row_count, slot_count * HD), w_out, preferred_element_type=jnp.float32
    )
    head_total = tp_sum(head_part)
    hidden = (tokens.astype(jnp.float32) + head_total).astype(jnp.bfloat16)
    mlp_in = rms_scale(hidden, mlp_gain)
    gate_part = jnp.dot(mlp_in, w_gate, preferred_element_type=jnp.float32)
    up_part = jnp.dot(mlp_in, w_up, preferred_element_type=jnp.float32)
    activation = (jax.nn.silu(gate_part) * up_part).astype(jnp.bfloat16)
    down_part = jnp.dot(activation, w_down, preferred_element_type=jnp.float32)
    down_total = tp_sum(down_part)
    return (hidden.astype(jnp.float32) + down_total).astype(jnp.bfloat16)


def solution(mesh):
    return jax.shard_map(
        on_device,
        mesh=mesh,
        in_specs=(
            P("seq", None),
            P(),
            P(None, "tp"),
            P(),
            P(),
            P("tp", None),
            P(None, "seq", None),
            P(None, "seq", None),
            P("seq", None, None),
            P("seq", None, None),
            P(),
            P(),
            P(),
            P(),
            P(None, "tp"),
            P(None, "tp"),
            P("tp", None),
        ),
        out_specs=P("seq", None),
        check_vma=False,
    )
```

```python
import functools

import jax
import numpy as np
import jax.numpy as jnp
from jax import lax
from jax.experimental import pallas as pl
from jax.experimental.pallas import tpu as pltpu
from jax.sharding import PartitionSpec as P

HEADS = 18
KV_HEADS = 6
HD = 64


NEG_FILL = -1e30
TILE = 64


def split_parts(values, count):
    parts = []
    for _ in range(count - 1):
        high = values.astype(jnp.bfloat16).astype(jnp.float32)
        parts.append(high)
        values = values - high
    parts.append(values.astype(jnp.bfloat16).astype(jnp.float32))
    return parts


def pair_window(tp_count, slot_count, width):
    spans = []
    for device_tp in range(tp_count):
        per_device = HEADS // tp_count
        start_head = per_device * device_tp + min(device_tp, HEADS % tp_count)
        heads = np.minimum(start_head + np.arange(slot_count), HEADS - 1) // (HEADS // KV_HEADS)
        spans.append(heads.max() // 2 - heads.min() // 2 + 1)
    return int(min(max(spans), width // 128))


def prefix_kernel(tile_of, group_at, valid, limit, kv, perm_ref, sg_ref, q_ref, k_ref, v_ref, o_ref, *, window):
    step = pl.program_id(0)
    tile = tile_of[step]
    first = jnp.logical_or(step == 0, tile_of[jnp.maximum(step - 1, 0)] != tile)
    rows, width = o_ref.shape
    lanes = 128
    slot_count = kv.shape[0]
    tail_at = (slot_count // 2) * lanes
    wide_lane = lax.broadcasted_iota(jnp.int32, (rows, width), 1)

    @pl.when(first)
    def _():
        top_lanes = jnp.logical_and(wide_lane >= tail_at + HD, wide_lane < tail_at + HD + slot_count)
        o_ref[...] = jnp.where(top_lanes, NEG_FILL, 0.0).astype(o_ref.dtype)

    group = group_at[step]
    live_count = limit[group]

    @pl.when(jnp.logical_and(valid[step] == 1, live_count > 0))
    def _():
        request_count = q_ref.shape[0]
        pick = (perm_ref[...] == lax.broadcasted_iota(jnp.int32, (rows, request_count), 1)).astype(jnp.bfloat16)
        q_rows = jnp.dot(pick, q_ref[...], preferred_element_type=jnp.float32)
        row_live = sg_ref[...] == group
        lane = lax.broadcasted_iota(jnp.int32, (rows, lanes), 1)
        upper = lane >= HD
        tile_total = window
        base = kv[0] // 2
        for slot in range(1, slot_count):
            base = jnp.minimum(base, kv[slot] // 2)
        base = jnp.minimum(base, width // lanes - window)
        start = pl.multiple_of(base * lanes, lanes)
        padded = []
        for slot in range(slot_count):
            head = kv[slot]
            odd = head % 2 == 1
            half = slot % 2 == 1
            block = q_rows[:, (slot // 2) * lanes : (slot // 2 + 1) * lanes]
            block = jnp.where(upper == half, block, 0.0)
            block = jnp.where(odd == half, block, pltpu.roll(block, HD, 1))
            padded.append(
                jnp.concatenate(
                    [jnp.where(head // 2 - base == j, block, 0.0) for j in range(tile_total)], axis=1
                ).astype(jnp.bfloat16)
            )
        padded = jnp.concatenate(padded, axis=0)
        scores = lax.dot_general(
            padded, k_ref[0, :, pl.ds(start, window * lanes)], (((1,), (1,)), ((), ())), preferred_element_type=jnp.float32
        ) * (HD ** (-0.5))
        spots = lax.broadcasted_iota(jnp.int32, scores.shape, 1)
        masked = jnp.where(spots < live_count, scores, NEG_FILL)
        top = jnp.max(masked, axis=1, keepdims=True)
        weights = jnp.exp(masked - top)
        total = jnp.sum(weights, axis=1, keepdims=True)
        mixed = jnp.dot(
            weights.astype(jnp.bfloat16), v_ref[0, :, pl.ds(start, window * lanes)], preferred_element_type=jnp.float32
        )
        pieces = []
        for slot in range(slot_count):
            head = kv[slot]
            odd = head % 2 == 1
            half = slot % 2 == 1
            mine = mixed[slot * rows : (slot + 1) * rows]
            chosen = mine[:, 0:lanes]
            for j in range(1, tile_total):
                chosen = jnp.where(head // 2 - base == j, mine[:, j * lanes : (j + 1) * lanes], chosen)
            pieces.append(jnp.where(odd == half, chosen, pltpu.roll(chosen, HD, 1)))
        if slot_count % 2:
            pieces.append(jnp.zeros((rows, lanes), jnp.float32))
        out = [jnp.where(upper, pieces[i + 1], pieces[i]) for i in range(0, len(pieces), 2)]
        tail = out[-1]
        parts = split_parts(top, 3) + split_parts(total, 3)
        for index, part in enumerate(parts):
            for slot in range(slot_count):
                tail = jnp.where(lane == HD + index * slot_count + slot, part[slot * rows : (slot + 1) * rows], tail)
        out[-1] = tail
        o_ref[...] = jnp.where(row_live, jnp.concatenate(out, axis=1).astype(o_ref.dtype), o_ref[...])


def prefix_partials(every_query, group_of, prefix_len, seq_index, prefix_keys, prefix_values, kv_ids, tp_count):
    request_count, width = every_query.shape
    group_count, prefix_span, _ = prefix_keys.shape
    tile_count = request_count // TILE
    visit_count = tile_count + group_count - 1
    order_key = group_of * request_count + jnp.arange(request_count, dtype=jnp.int32)
    rank = jnp.sum((order_key[None, :] < order_key[:, None]).astype(jnp.int32), axis=1)
    spots = jnp.arange(request_count, dtype=jnp.int32)
    match = rank[None, :] == spots[:, None]
    perm = jnp.sum(jnp.where(match, spots[None, :], 0), axis=1)
    sorted_groups = jnp.sum(jnp.where(match, group_of[None, :], 0), axis=1)
    low = sorted_groups[0::TILE]
    high = sorted_groups[TILE - 1 :: TILE]
    spans = high - low + 1
    ends = jnp.cumsum(spans)
    starts = ends - spans
    visits = jnp.arange(visit_count, dtype=jnp.int32)
    tile_of = jnp.minimum(jnp.sum((ends[None, :] <= visits[:, None]).astype(jnp.int32), axis=1), tile_count - 1)
    valid = (visits < ends[-1]).astype(jnp.int32)
    group_at = jnp.where(valid == 1, jnp.take(low, tile_of) + visits - jnp.take(starts, tile_of), high[-1])
    limit = jnp.clip(prefix_len - seq_index * prefix_span, 0, prefix_span).astype(jnp.int32)
    slot_count = kv_ids.shape[0]
    grid_spec = pltpu.PrefetchScalarGridSpec(
        num_scalar_prefetch=5,
        grid=(visit_count,),
        in_specs=[
            pl.BlockSpec((TILE, 1), lambda i, t, g, ok, lim, kv: (t[i], 0)),
            pl.BlockSpec((TILE, 1), lambda i, t, g, ok, lim, kv: (t[i], 0)),
            pl.BlockSpec((request_count, width), lambda i, t, g, ok, lim, kv: (0, 0)),
            pl.BlockSpec((1, prefix_span, width), lambda i, t, g, ok, lim, kv: (g[i], 0, 0)),
            pl.BlockSpec((1, prefix_span, width), lambda i, t, g, ok, lim, kv: (g[i], 0, 0)),
        ],
        out_specs=pl.BlockSpec((TILE, width), lambda i, t, g, ok, lim, kv: (t[i], 0)),
    )
    lanes = 128
    flops = visit_count * (2 * TILE * request_count * width + slot_count * 4 * TILE * width * prefix_span)
    window = pair_window(tp_count, slot_count, width)
    out = pl.pallas_call(
        functools.partial(prefix_kernel, window=window),
        grid_spec=grid_spec,
        out_shape=jax.ShapeDtypeStruct((request_count, width), jnp.bfloat16),
        compiler_params=pltpu.CompilerParams(dimension_semantics=("arbitrary",)),
        cost_estimate=pl.CostEstimate(
            flops=flops,
            transcendentals=visit_count * TILE * slot_count * prefix_span,
            bytes_accessed=visit_count * 2 * prefix_span * width * 2 + request_count * width * 6,
        ),
    )(
        tile_of,
        group_at,
        valid,
        limit,
        kv_ids,
        perm.reshape(-1, 1),
        sorted_groups.reshape(-1, 1),
        every_query,
        prefix_keys,
        prefix_values,
    )
    unsort = (rank[:, None] == spots[None, :]).astype(jnp.bfloat16)
    return jnp.dot(unsort, out, preferred_element_type=jnp.float32).astype(jnp.bfloat16)


def rms_scale(values_in, gain_row):
    widened = values_in.astype(jnp.float32)
    factor = lax.rsqrt(jnp.mean(widened * widened, axis=-1, keepdims=True) + 1e-05)
    return (widened * factor * gain_row).astype(jnp.bfloat16)


def rotate_heads(blocks, position):
    half_dim = blocks.shape[-1] // 2
    frequency = jnp.power(10000.0, -jnp.arange(half_dim, dtype=jnp.float32) / half_dim)
    angles = position.astype(jnp.float32)[:, None, None] * frequency
    cosine = jnp.cos(angles)
    sine_part = jnp.sin(angles)
    low_half = blocks[..., :half_dim]
    high_half = blocks[..., half_dim:]
    return jnp.concatenate(
        [low_half * cosine - high_half * sine_part, high_half * cosine + low_half * sine_part],
        axis=-1,
    )


def slot_layout(device_tp, tp_count, slot_count):
    per_device = HEADS // tp_count
    surplus = HEADS % tp_count
    start_head = per_device * device_tp + jnp.minimum(device_tp, surplus)
    used_count = per_device + (device_tp < surplus).astype(jnp.int32)
    slot_ids = jnp.arange(slot_count, dtype=jnp.int32)
    head_ids = start_head + slot_ids
    slot_used = (slot_ids < used_count).astype(jnp.float32)
    kv_ids = jnp.minimum(head_ids, HEADS - 1) // (HEADS // KV_HEADS)
    return (kv_ids, slot_used)


def tp_sum(part):
    sent = part.astype(jnp.bfloat16)
    count = lax.axis_size("tp")
    total = sent.astype(jnp.float32)
    for shift in range(1, count):
        moved = lax.ppermute(sent, "tp", [(j, (j + shift) % count) for j in range(count)])
        total = total + moved.astype(jnp.float32)
    return total


def on_device(
    tokens,
    attn_gain,
    w_query,
    w_key,
    w_value,
    w_out,
    prefix_keys,
    prefix_values,
    suffix_keys,
    suffix_values,
    group_of,
    prefix_len,
    suffix_len,
    mlp_gain,
    w_gate,
    w_up,
    w_down,
):
    row_count = tokens.shape[0]
    slot_count = w_query.shape[1] // HD
    group_count = prefix_keys.shape[0]
    prefix_span = prefix_keys.shape[1]
    suffix_span = suffix_keys.shape[1]
    seq_index = lax.axis_index("seq")
    kv_ids, slot_used = slot_layout(lax.axis_index("tp"), lax.axis_size("tp"), slot_count)
    normed = rms_scale(tokens, attn_gain)
    queries = jnp.dot(normed, w_query, preferred_element_type=jnp.float32).reshape(
        row_count, slot_count, HD
    )
    new_keys = jnp.dot(normed, w_key, preferred_element_type=jnp.float32).reshape(
        row_count, KV_HEADS, HD
    )
    new_values = (
        jnp.dot(normed, w_value, preferred_element_type=jnp.float32)
        .astype(jnp.bfloat16)
        .reshape(row_count, KV_HEADS, HD)
    )
    own_start = seq_index * row_count
    own_groups = lax.dynamic_slice_in_dim(group_of, own_start, row_count)
    own_suffix = lax.dynamic_slice_in_dim(suffix_len, own_start, row_count)
    group_ids = jnp.arange(group_count, dtype=jnp.int32)
    own_prefix = jnp.sum(
        jnp.where(own_groups[:, None] == group_ids[None, :], prefix_len[None, :], 0), axis=1
    )
    position = own_prefix + own_suffix
    queries = rotate_heads(queries, position).astype(jnp.bfloat16)
    new_keys = rotate_heads(new_keys, position).astype(jnp.bfloat16)
    seq_count = lax.axis_size("seq")
    query_width = prefix_keys.shape[2]
    own_query = jnp.pad(
        queries.reshape(1, row_count, slot_count * HD),
        ((0, 0), (0, 0), (0, query_width - slot_count * HD)),
    )
    every_query = lax.all_to_all(
        jnp.broadcast_to(own_query, (seq_count, row_count, query_width)),
        "seq",
        0,
        0,
        tiled=True,
    )
    every_query = every_query.reshape(-1, query_width)
    score_scale = HD ** (-0.5)
    payload = prefix_partials(
        every_query, group_of, prefix_len, seq_index, prefix_keys, prefix_values, kv_ids, lax.axis_size("tp")
    )
    payload = payload.reshape(seq_count, row_count, query_width)
    gathered = lax.all_to_all(payload, "seq", 0, 0, tiled=True).astype(jnp.float32)
    tail_at = (slot_count // 2) * 128 + HD
    tail_parts = [gathered[..., tail_at + i * slot_count : tail_at + (i + 1) * slot_count] for i in range(6)]
    gathered_top = (tail_parts[0] + tail_parts[1]) + tail_parts[2]
    gathered_total = (tail_parts[3] + tail_parts[4]) + tail_parts[5]
    gathered_mixed = gathered[..., : slot_count * HD].reshape(seq_count, row_count, slot_count, HD)
    part_top = jnp.max(gathered_top, axis=0)
    part_scale = jnp.exp(gathered_top - part_top[None])
    part_total = jnp.sum(part_scale * gathered_total, axis=0)
    part_mixed = jnp.sum(part_scale[..., None] * gathered_mixed, axis=0)
    suf_keys = jnp.take(suffix_keys.reshape(row_count, suffix_span, KV_HEADS, HD), kv_ids, axis=2)
    suf_values = jnp.take(
        suffix_values.reshape(row_count, suffix_span, KV_HEADS, HD), kv_ids, axis=2
    )
    suf_scores = (
        jnp.einsum("rsd,rjsd->rsj", queries, suf_keys, preferred_element_type=jnp.float32)
        * score_scale
    )
    suf_live = (jnp.arange(suffix_span, dtype=jnp.int32)[None, :] < own_suffix[:, None])[:, None, :]
    suf_top = jnp.max(jnp.where(suf_live, suf_scores, NEG_FILL), axis=2)
    own_keys = jnp.take(new_keys, kv_ids, axis=1).astype(jnp.float32)
    own_values = jnp.take(new_values, kv_ids, axis=1).astype(jnp.float32)
    own_score = jnp.sum(queries.astype(jnp.float32) * own_keys, axis=-1) * score_scale
    local_top = jnp.maximum(suf_top, own_score)
    suf_weights = jnp.where(suf_live, jnp.exp(suf_scores - local_top[:, :, None]), 0.0)
    own_weight = jnp.exp(own_score - local_top)
    local_total = jnp.sum(suf_weights, axis=2) + own_weight
    own_low = lax.optimization_barrier(own_weight.astype(jnp.bfloat16)).astype(jnp.float32)
    local_mixed = own_low[..., None] * own_values + jnp.einsum(
        "rsj,rjsd->rsd",
        suf_weights.astype(jnp.bfloat16),
        suf_values,
        preferred_element_type=jnp.float32,
    )
    final_top = jnp.maximum(part_top, local_top)
    carried = jnp.exp(part_top - final_top)
    kept = jnp.exp(local_top - final_top)
    denominator = carried * part_total + kept * local_total
    numerator = carried[..., None] * part_mixed + kept[..., None] * local_mixed
    attended = (numerator / denominator[..., None] * slot_used[None, :, None]).astype(jnp.bfloat16)
    head_part = jnp.dot(
        attended.reshape(row_count, slot_count * HD), w_out, preferred_element_type=jnp.float32
    )
    head_total = tp_sum(head_part)
    hidden = (tokens.astype(jnp.float32) + head_total).astype(jnp.bfloat16)
    mlp_in = rms_scale(hidden, mlp_gain)
    gate_part = jnp.dot(mlp_in, w_gate, preferred_element_type=jnp.float32)
    up_part = jnp.dot(mlp_in, w_up, preferred_element_type=jnp.float32)
    activation = (jax.nn.silu(gate_part) * up_part).astype(jnp.bfloat16)
    down_part = jnp.dot(activation, w_down, preferred_element_type=jnp.float32)
    down_total = tp_sum(down_part)
    return (hidden.astype(jnp.float32) + down_total).astype(jnp.bfloat16)


def solution(mesh):
    return jax.shard_map(
        on_device,
        mesh=mesh,
        in_specs=(
            P("seq", None),
            P(),
            P(None, "tp"),
            P(),
            P(),
            P("tp", None),
            P(None, "seq", None),
            P(None, "seq", None),
            P("seq", None, None),
            P("seq", None, None),
            P(),
            P(),
            P(),
            P(),
            P(None, "tp"),
            P(None, "tp"),
            P("tp", None),
        ),
        out_specs=P("seq", None),
        check_vma=False,
    )
```

```python
import functools

import jax
import numpy as np
import jax.numpy as jnp
from jax import lax
from jax.experimental import pallas as pl
from jax.experimental.pallas import tpu as pltpu
from jax.sharding import PartitionSpec as P


HEADS = 18
KV_HEADS = 6
HD = 64


NEG_FILL = -1e30
TILE = 64


def split_parts(values, count):
    parts = []
    for _ in range(count - 1):
        high = values.astype(jnp.bfloat16).astype(jnp.float32)
        parts.append(high)
        values = values - high
    parts.append(values.astype(jnp.bfloat16).astype(jnp.float32))
    return parts


def pair_window(tp_count, slot_count, width):
    spans = []
    for device_tp in range(tp_count):
        per_device = HEADS // tp_count
        start_head = per_device * device_tp + min(device_tp, HEADS % tp_count)
        heads = np.minimum(start_head + np.arange(slot_count), HEADS - 1) // (HEADS // KV_HEADS)
        spans.append(heads.max() // 2 - heads.min() // 2 + 1)
    return int(min(max(spans), width // 128))


def prefix_kernel(tile_of, group_at, valid, limit, kv, perm_ref, sg_ref, q_ref, k_ref, v_ref, o_ref, *, window):
    step = pl.program_id(0)
    tile = tile_of[step]
    first = jnp.logical_or(step == 0, tile_of[jnp.maximum(step - 1, 0)] != tile)
    rows, width = o_ref.shape
    lanes = 128
    slot_count = kv.shape[0]
    tail_at = (slot_count // 2) * lanes
    wide_lane = lax.broadcasted_iota(jnp.int32, (rows, width), 1)

    @pl.when(first)
    def _():
        top_lanes = jnp.logical_and(wide_lane >= tail_at + HD, wide_lane < tail_at + HD + slot_count)
        o_ref[...] = jnp.where(top_lanes, NEG_FILL, 0.0).astype(o_ref.dtype)

    group = group_at[step]
    live_count = limit[group]

    @pl.when(jnp.logical_and(valid[step] == 1, live_count > 0))
    def _():
        request_count = q_ref.shape[0]
        pick = (perm_ref[...] == lax.broadcasted_iota(jnp.int32, (rows, request_count), 1)).astype(jnp.bfloat16)
        q_rows = jnp.dot(pick, q_ref[...], preferred_element_type=jnp.float32)
        row_live = sg_ref[...] == group
        lane = lax.broadcasted_iota(jnp.int32, (rows, lanes), 1)
        upper = lane >= HD
        tile_total = window
        base = kv[0] // 2
        for slot in range(1, slot_count):
            base = jnp.minimum(base, kv[slot] // 2)
        base = jnp.minimum(base, width // lanes - window)
        start = pl.multiple_of(base * lanes, lanes)
        padded = []
        for slot in range(slot_count):
            head = kv[slot]
            odd = head % 2 == 1
            half = slot % 2 == 1
            block = q_rows[:, (slot // 2) * lanes : (slot // 2 + 1) * lanes]
            block = jnp.where(upper == half, block, 0.0)
            block = jnp.where(odd == half, block, pltpu.roll(block, HD, 1))
            padded.append(
                jnp.concatenate(
                    [jnp.where(head // 2 - base == j, block, 0.0) for j in range(tile_total)], axis=1
                ).astype(jnp.bfloat16)
            )
        padded = jnp.concatenate(padded, axis=0)
        scores = lax.dot_general(
            padded, k_ref[0, :, pl.ds(start, window * lanes)], (((1,), (1,)), ((), ())), preferred_element_type=jnp.float32
        ) * (HD ** (-0.5))
        spots = lax.broadcasted_iota(jnp.int32, scores.shape, 1)
        masked = jnp.where(spots < live_count, scores, NEG_FILL)
        top = jnp.max(masked, axis=1, keepdims=True)
        weights = jnp.exp(masked - top)
        total = jnp.sum(weights, axis=1, keepdims=True)
        mixed = jnp.dot(
            weights.astype(jnp.bfloat16), v_ref[0, :, pl.ds(start, window * lanes)], preferred_element_type=jnp.float32
        )
        pieces = []
        for slot in range(slot_count):
            head = kv[slot]
            odd = head % 2 == 1
            half = slot % 2 == 1
            mine = mixed[slot * rows : (slot + 1) * rows]
            chosen = mine[:, 0:lanes]
            for j in range(1, tile_total):
                chosen = jnp.where(head // 2 - base == j, mine[:, j * lanes : (j + 1) * lanes], chosen)
            pieces.append(jnp.where(odd == half, chosen, pltpu.roll(chosen, HD, 1)))
        if slot_count % 2:
            pieces.append(jnp.zeros((rows, lanes), jnp.float32))
        out = [jnp.where(upper, pieces[i + 1], pieces[i]) for i in range(0, len(pieces), 2)]
        tail = out[-1]
        parts = split_parts(top, 3) + split_parts(total, 3)
        for index, part in enumerate(parts):
            for slot in range(slot_count):
                tail = jnp.where(lane == HD + index * slot_count + slot, part[slot * rows : (slot + 1) * rows], tail)
        out[-1] = tail
        o_ref[...] = jnp.where(row_live, jnp.concatenate(out, axis=1).astype(o_ref.dtype), o_ref[...])


def prefix_partials(every_query, group_of, prefix_len, seq_index, prefix_keys, prefix_values, kv_ids, tp_count):
    request_count, width = every_query.shape
    group_count, prefix_span, _ = prefix_keys.shape
    tile_count = request_count // TILE
    visit_count = tile_count + group_count - 1
    order_key = group_of * request_count + jnp.arange(request_count, dtype=jnp.int32)
    rank = jnp.sum((order_key[None, :] < order_key[:, None]).astype(jnp.int32), axis=1)
    spots = jnp.arange(request_count, dtype=jnp.int32)
    match = rank[None, :] == spots[:, None]
    perm = jnp.sum(jnp.where(match, spots[None, :], 0), axis=1)
    sorted_groups = jnp.sum(jnp.where(match, group_of[None, :], 0), axis=1)
    low = sorted_groups[0::TILE]
    high = sorted_groups[TILE - 1 :: TILE]
    spans = high - low + 1
    ends = jnp.cumsum(spans)
    starts = ends - spans
    visits = jnp.arange(visit_count, dtype=jnp.int32)
    tile_of = jnp.minimum(jnp.sum((ends[None, :] <= visits[:, None]).astype(jnp.int32), axis=1), tile_count - 1)
    valid = (visits < ends[-1]).astype(jnp.int32)
    group_at = jnp.where(valid == 1, jnp.take(low, tile_of) + visits - jnp.take(starts, tile_of), high[-1])
    limit = jnp.clip(prefix_len - seq_index * prefix_span, 0, prefix_span).astype(jnp.int32)
    slot_count = kv_ids.shape[0]
    grid_spec = pltpu.PrefetchScalarGridSpec(
        num_scalar_prefetch=5,
        grid=(visit_count,),
        in_specs=[
            pl.BlockSpec((TILE, 1), lambda i, t, g, ok, lim, kv: (t[i], 0)),
            pl.BlockSpec((TILE, 1), lambda i, t, g, ok, lim, kv: (t[i], 0)),
            pl.BlockSpec((request_count, width), lambda i, t, g, ok, lim, kv: (0, 0)),
            pl.BlockSpec((1, prefix_span, width), lambda i, t, g, ok, lim, kv: (g[i], 0, 0)),
            pl.BlockSpec((1, prefix_span, width), lambda i, t, g, ok, lim, kv: (g[i], 0, 0)),
        ],
        out_specs=pl.BlockSpec((TILE, width), lambda i, t, g, ok, lim, kv: (t[i], 0)),
    )
    flops = visit_count * (2 * TILE * request_count * width + slot_count * 4 * TILE * width * prefix_span)
    window = pair_window(tp_count, slot_count, width)
    out = pl.pallas_call(
        functools.partial(prefix_kernel, window=window),
        grid_spec=grid_spec,
        out_shape=jax.ShapeDtypeStruct((request_count, width), jnp.bfloat16),
        compiler_params=pltpu.CompilerParams(dimension_semantics=("arbitrary",)),
        cost_estimate=pl.CostEstimate(
            flops=flops,
            transcendentals=visit_count * TILE * slot_count * prefix_span,
            bytes_accessed=visit_count * 2 * prefix_span * width * 2 + request_count * width * 6,
        ),
    )(
        tile_of,
        group_at,
        valid,
        limit,
        kv_ids,
        perm.reshape(-1, 1),
        sorted_groups.reshape(-1, 1),
        every_query,
        prefix_keys,
        prefix_values,
    )
    unsort = (rank[:, None] == spots[None, :]).astype(jnp.bfloat16)
    return jnp.dot(unsort, out, preferred_element_type=jnp.float32).astype(jnp.bfloat16)


def rms_scale(values_in, gain_row):
    widened = values_in.astype(jnp.float32)
    factor = lax.rsqrt(jnp.mean(widened * widened, axis=-1, keepdims=True) + 1e-05)
    return (widened * factor * gain_row).astype(jnp.bfloat16)


def rotate_heads(blocks, position):
    half_dim = blocks.shape[-1] // 2
    frequency = jnp.power(10000.0, -jnp.arange(half_dim, dtype=jnp.float32) / half_dim)
    angles = position.astype(jnp.float32)[:, None, None] * frequency
    cosine = jnp.cos(angles)
    sine_part = jnp.sin(angles)
    low_half = blocks[..., :half_dim]
    high_half = blocks[..., half_dim:]
    return jnp.concatenate(
        [low_half * cosine - high_half * sine_part, high_half * cosine + low_half * sine_part],
        axis=-1,
    )


def slot_layout(device_tp, tp_count, slot_count):
    per_device = HEADS // tp_count
    surplus = HEADS % tp_count
    start_head = per_device * device_tp + jnp.minimum(device_tp, surplus)
    used_count = per_device + (device_tp < surplus).astype(jnp.int32)
    slot_ids = jnp.arange(slot_count, dtype=jnp.int32)
    head_ids = start_head + slot_ids
    slot_used = (slot_ids < used_count).astype(jnp.float32)
    kv_ids = jnp.minimum(head_ids, HEADS - 1) // (HEADS // KV_HEADS)
    return (kv_ids, slot_used)


def tp_sum(part):
    sent = part.astype(jnp.bfloat16)
    count = lax.axis_size("tp")
    total = sent.astype(jnp.float32)
    for shift in range(1, count):
        moved = lax.ppermute(sent, "tp", [(j, (j + shift) % count) for j in range(count)])
        total = total + moved.astype(jnp.float32)
    return total


def on_device(
    tokens,
    attn_gain,
    w_query,
    w_key,
    w_value,
    w_out,
    prefix_keys,
    prefix_values,
    suffix_keys,
    suffix_values,
    group_of,
    prefix_len,
    suffix_len,
    mlp_gain,
    w_gate,
    w_up,
    w_down,
):
    row_count = tokens.shape[0]
    slot_count = w_query.shape[1] // HD
    group_count = prefix_keys.shape[0]
    suffix_span = suffix_keys.shape[1]
    seq_index = lax.axis_index("seq")
    kv_ids, slot_used = slot_layout(lax.axis_index("tp"), lax.axis_size("tp"), slot_count)
    normed = rms_scale(tokens, attn_gain)
    queries = jnp.dot(normed, w_query, preferred_element_type=jnp.float32).reshape(
        row_count, slot_count, HD
    )
    own_start = seq_index * row_count
    own_groups = lax.dynamic_slice_in_dim(group_of, own_start, row_count)
    own_suffix = lax.dynamic_slice_in_dim(suffix_len, own_start, row_count)
    group_ids = jnp.arange(group_count, dtype=jnp.int32)
    own_prefix = jnp.sum(
        jnp.where(own_groups[:, None] == group_ids[None, :], prefix_len[None, :], 0), axis=1
    )
    position = own_prefix + own_suffix
    queries = rotate_heads(queries, position).astype(jnp.bfloat16)
    seq_count = lax.axis_size("seq")
    query_width = prefix_keys.shape[2]
    own_query = jnp.pad(
        queries.reshape(1, row_count, slot_count * HD),
        ((0, 0), (0, 0), (0, query_width - slot_count * HD)),
    )
    every_query = lax.all_to_all(
        jnp.broadcast_to(own_query, (seq_count, row_count, query_width)),
        "seq",
        0,
        0,
        tiled=True,
    )
    every_query = every_query.reshape(-1, query_width)
    score_scale = HD ** (-0.5)
    payload = prefix_partials(
        every_query, group_of, prefix_len, seq_index, prefix_keys, prefix_values, kv_ids, lax.axis_size("tp")
    )
    payload = payload.reshape(seq_count, row_count, query_width)
    late_normed, payload = lax.optimization_barrier((normed, payload))
    new_keys = jnp.dot(late_normed, w_key, preferred_element_type=jnp.float32).reshape(
        row_count, KV_HEADS, HD
    )
    new_values = (
        jnp.dot(late_normed, w_value, preferred_element_type=jnp.float32)
        .astype(jnp.bfloat16)
        .reshape(row_count, KV_HEADS, HD)
    )
    new_keys = rotate_heads(new_keys, position).astype(jnp.bfloat16)
    gathered = lax.all_to_all(payload, "seq", 0, 0, tiled=True)
    gathered = gathered.astype(jnp.float32)
    tail_at = (slot_count // 2) * 128 + HD
    tail_parts = [gathered[..., tail_at + i * slot_count : tail_at + (i + 1) * slot_count] for i in range(6)]
    gathered_top = (tail_parts[0] + tail_parts[1]) + tail_parts[2]
    gathered_total = (tail_parts[3] + tail_parts[4]) + tail_parts[5]
    gathered_mixed = gathered[..., : slot_count * HD].reshape(seq_count, row_count, slot_count, HD)
    part_top = jnp.max(gathered_top, axis=0)
    part_scale = jnp.exp(gathered_top - part_top[None])
    part_total = jnp.sum(part_scale * gathered_total, axis=0)
    part_mixed = jnp.sum(part_scale[..., None] * gathered_mixed, axis=0)
    suf_keys = jnp.take(suffix_keys.reshape(row_count, suffix_span, KV_HEADS, HD), kv_ids, axis=2)
    suf_values = jnp.take(
        suffix_values.reshape(row_count, suffix_span, KV_HEADS, HD), kv_ids, axis=2
    )
    suf_scores = (
        jnp.einsum("rsd,rjsd->rsj", queries, suf_keys, preferred_element_type=jnp.float32)
        * score_scale
    )
    suf_live = (jnp.arange(suffix_span, dtype=jnp.int32)[None, :] < own_suffix[:, None])[:, None, :]
    suf_top = jnp.max(jnp.where(suf_live, suf_scores, NEG_FILL), axis=2)
    own_keys = jnp.take(new_keys, kv_ids, axis=1).astype(jnp.float32)
    own_values = jnp.take(new_values, kv_ids, axis=1).astype(jnp.float32)
    own_score = jnp.sum(queries.astype(jnp.float32) * own_keys, axis=-1) * score_scale
    local_top = jnp.maximum(suf_top, own_score)
    suf_weights = jnp.where(suf_live, jnp.exp(suf_scores - local_top[:, :, None]), 0.0)
    own_weight = jnp.exp(own_score - local_top)
    local_total = jnp.sum(suf_weights, axis=2) + own_weight
    own_low = lax.optimization_barrier(own_weight.astype(jnp.bfloat16)).astype(jnp.float32)
    local_mixed = own_low[..., None] * own_values + jnp.einsum(
        "rsj,rjsd->rsd",
        suf_weights.astype(jnp.bfloat16),
        suf_values,
        preferred_element_type=jnp.float32,
    )
    final_top = jnp.maximum(part_top, local_top)
    carried = jnp.exp(part_top - final_top)
    kept = jnp.exp(local_top - final_top)
    denominator = carried * part_total + kept * local_total
    numerator = carried[..., None] * part_mixed + kept[..., None] * local_mixed
    attended = (numerator / denominator[..., None] * slot_used[None, :, None]).astype(jnp.bfloat16)
    head_part = jnp.dot(
        attended.reshape(row_count, slot_count * HD), w_out, preferred_element_type=jnp.float32
    )
    head_total = tp_sum(head_part)
    hidden = (tokens.astype(jnp.float32) + head_total).astype(jnp.bfloat16)
    mlp_in = rms_scale(hidden, mlp_gain)
    gate_part = jnp.dot(mlp_in, w_gate, preferred_element_type=jnp.float32)
    up_part = jnp.dot(mlp_in, w_up, preferred_element_type=jnp.float32)
    activation = (jax.nn.silu(gate_part) * up_part).astype(jnp.bfloat16)
    down_part = jnp.dot(activation, w_down, preferred_element_type=jnp.float32)
    down_total = tp_sum(down_part)
    return (hidden.astype(jnp.float32) + down_total).astype(jnp.bfloat16)


def solution(mesh):
    return jax.shard_map(
        on_device,
        mesh=mesh,
        in_specs=(
            P("seq", None),
            P(),
            P(None, "tp"),
            P(),
            P(),
            P("tp", None),
            P(None, "seq", None),
            P(None, "seq", None),
            P("seq", None, None),
            P("seq", None, None),
            P(),
            P(),
            P(),
            P(),
            P(None, "tp"),
            P(None, "tp"),
            P("tp", None),
        ),
        out_specs=P("seq", None),
        check_vma=False,
    )
```
